32 devices in a mesh: group: 2 (over core), gx: 4 (over y, x), gy: 4 (over z).
Axes of the slice: x: 2, y: 2, z: 4, core: 2. Of those that a mesh axis runs over, the one named last changes fastest.
Arguments:
- gradient_windows: bfloat16 [2, 4, 4, 256, 4, 2, 128], P('group', 'gx', 'gy'), may hold values from -6 to 6
- illumination_windows: bfloat16 [2, 4, 4, 256, 4, 2, 128], P('group', 'gx', 'gy'), may hold values from 0.25 to 8
- window_owners: int32 [2, 4, 4, 256], P('group', 'gx', 'gy'), may hold values from 0 to 15, as said below
- window_patches: int32 [2, 4, 4, 256], P('group', 'gx', 'gy'), may hold values from 0 to 7
- velocity: float32 [4, 64, 512], P(None, 'gx', 'gy'), may hold values from 1.5 to 4.5
Outputs:
- updated_model: float32 [4, 64, 512], P(None, 'gx', 'gy')
- returned_windows: bfloat16 [2, 4, 4, 256, 4, 2, 128], P('group', 'gx', 'gy')
The draws below stay inside these ranges and needn't reach their ends.
Inputs may be any that keep to these rules, and one draw needn't show every extreme that they name: `window_owners`: the window patches of one device name any tile at most 20 times; one tile is named exactly 20 times by the window patches of every device.
All inputs are finite; a program needn't handle non-finite values.
Results may differ from the reference program's by a relative error of at most 0.001.
Values may be sent and summed in bfloat16 or wider, within the bound.
No kernel may reach another device: no remote copies, remote signals or barrier semaphores. Data moves between devices by JAX's collectives and lax.ppermute only.
A program may use at most 64 MiB of HBM per device.

```python
import math
import jax
import jax.numpy as jnp
from jax import lax

LEV = 4
PX = 2
PY = 128
PPT = 8
SLOTS = 256
SWEEPS = 4
CAP = 20
NX = 64
NY = 512
N_GROUP = 2
N_GX = 4
N_GY = 4


def draw_window_owners(key, part):
    holder_count = N_GX * N_GY
    sources = N_GROUP * N_GX * N_GY
    table_entries = holder_count * CAP
    entry_holder_index = jnp.arange(table_entries, dtype=jnp.int32) // CAP
    frequent_owner = jax.random.randint(jax.random.fold_in(key, 1), (holder_count,), 0, 3)
    selected_owner = jax.random.randint(jax.random.fold_in(key, 2), (), 0, holder_count)
    extra_priority_level = jnp.where(jnp.arange(holder_count) == selected_owner, 8, frequent_owner)[entry_holder_index]

    def one_source(source_index):
        source_key = jax.random.fold_in(jax.random.fold_in(key, 3), source_index)
        random_jitter_values = jax.random.randint(source_key, (table_entries,), 0, 4096)
        ranking_scores = ((extra_priority_level * 4096 + random_jitter_values) * table_entries + jnp.arange(table_entries)).astype(jnp.int32)
        top_vals, picked = lax.top_k(ranking_scores, SLOTS)
        shuffle = jax.random.permutation(jax.random.fold_in(source_key, 1), SLOTS)
        return entry_holder_index[picked][shuffle]
    chosen_rows = jax.vmap(one_source)(jnp.arange(sources))
    return chosen_rows.reshape(N_GROUP, N_GX, N_GY, SLOTS).astype(jnp.int32)


def touch_ends(entries, own_key, low, top_value):
    dims = entries.shape
    place = [jax.random.randint(jax.random.fold_in(own_key, axis), (), 0, dims[axis]) for axis in range(len(dims))]
    entries = entries.at[tuple(place)].set(low)
    longest = dims.index(max(dims))
    place[longest] = (place[longest] + 1) % dims[longest]
    return entries.at[tuple(place)].set(top_value)


def level_of(own_key, dims, shards, smallest, high):
    gain = 1.0
    for position, parts in shards:
        heights = jax.random.uniform(jax.random.fold_in(jax.random.fold_in(own_key, 6), position), (parts,), jnp.float32, smallest / len(shards), high / len(shards))
        gain = gain * jnp.repeat(jnp.exp(heights), dims[position] // parts).reshape((-1,) + (1,) * (len(dims) - 1 - position))
    return gain


def normal_values(rng, dims, spread, reach, pieces=(), kind=jnp.bfloat16):
    array = jax.random.normal(rng, dims, jnp.float32) * spread
    if len(pieces) > 0:
        array = level_of(rng, dims, pieces, -0.22, 0.18) * array
    return jnp.clip(array, min=-reach, max=reach).astype(kind)


def setup_inputs(seed: int = 0) -> dict:
    keys = jax.random.split(jax.random.key(seed), 6)
    return {
        "gradient_windows": normal_values(keys[0], (N_GROUP, N_GX, N_GY, SLOTS, LEV, PX, PY), 1.0, 6.0, ((0, 2), (1, 4), (2, 4))),
        "illumination_windows": jnp.clip(jnp.exp(math.log(8.0) - 3.465736 * jax.random.uniform(keys[1], (N_GROUP, N_GX, N_GY, SLOTS, LEV, PX, PY), jnp.float32) ** level_of(keys[1], (N_GROUP, N_GX, N_GY, SLOTS, LEV, PX, PY), ((0, 2), (1, 4), (2, 4)), -0.2, 0.2)), 0.25, 8.0).astype(jnp.bfloat16),
        "window_owners": draw_window_owners(jax.random.fold_in(keys[5], 71), 0),
        "window_patches": touch_ends(jax.random.randint(keys[3], (N_GROUP, N_GX, N_GY, SLOTS), 0, PPT), jax.random.fold_in(keys[3], 1), 0, PPT - 1).astype(jnp.int32),
        "velocity": jnp.clip(jnp.exp(math.log(4.5) - 1.0986123 * jax.random.uniform(keys[4], (LEV, NX, NY), jnp.float32) ** level_of(keys[4], (LEV, NX, NY), ((1, 4), (2, 4)), -0.2, 0.2)), 1.5, 4.5),
    }


damping = 10.0
smooth_rate = 0.12
step_length = 24.0


def reference(gradient_windows, illumination_windows, window_owners, window_patches, velocity):
    sources = N_GROUP * N_GX * N_GY
    holder_count = N_GX * N_GY
    cell_count = LEV * PX * PY
    grad_rows = gradient_windows.reshape(sources, SLOTS, cell_count)
    illum_rows = illumination_windows.reshape(sources, SLOTS, cell_count)
    index_rows = (window_owners * PPT + window_patches).reshape(sources, SLOTS).astype(jnp.int32)

    def accumulate(totals, slot_items):
        grad_part, illum_part, index_part = slot_items
        grad_total, illum_total = totals
        grad_total = grad_total.at[index_part].add(grad_part.astype(jnp.float32))
        illum_total = illum_total.at[index_part].add(illum_part.astype(jnp.float32))
        return (grad_total, illum_total), None

    empty = jnp.zeros((holder_count * PPT, cell_count), jnp.float32)
    (grad_total, illum_total), unused = lax.scan(accumulate, (empty, empty), (grad_rows, illum_rows, index_rows))

    def to_grid(patch_rows):
        return patch_rows.reshape(N_GX, N_GY, PPT, LEV, PX, PY).transpose(3, 0, 2, 4, 1, 5).reshape(LEV, N_GX * PPT * PX, N_GY * PY)

    precondition = to_grid(grad_total) / (to_grid(illum_total) + damping)
    field_now = precondition
    for sweep_index in range(SWEEPS):
        padded = jnp.pad(field_now, 1)
        beside = (padded[1:-1, 2:, 1:-1] + padded[1:-1, :-2, 1:-1]) + (padded[1:-1, 1:-1, 2:] + padded[1:-1, 1:-1, :-2]) + (padded[2:, 1:-1, 1:-1] + padded[:-2, 1:-1, 1:-1])
        field_now = field_now + smooth_rate * (beside - 6.0 * field_now)
    updated_model = velocity - step_length * field_now
    patch_table = updated_model.reshape(LEV, N_GX, PPT, PX, N_GY, PY).transpose(1, 4, 2, 0, 3, 5).reshape(holder_count * PPT, LEV, PX, PY)
    returned = jnp.take(patch_table, index_rows.reshape(-1), axis=0).astype(jnp.bfloat16)
    returned_windows = returned.reshape(N_GROUP, N_GX, N_GY, SLOTS, LEV, PX, PY)
    return (updated_model, returned_windows)
```

```python
import jax
import jax.numpy as jnp
from jax import lax
from jax.sharding import PartitionSpec as P

SWEEPS = 4
HALO = SWEEPS


damping = 10.0
smooth_rate = 0.12
step_length = 24.0


def shifted(value, axis, count, step):
    return lax.ppermute(value, axis, [(s, (s + step) % count) for s in range(count)])


def local(gradient_windows, illumination_windows, window_owners, window_patches, velocity):
    size_x = lax.axis_size("gx")
    size_y = lax.axis_size("gy")
    size_g = lax.axis_size("group")
    me_x = lax.axis_index("gx")
    me_y = lax.axis_index("gy")
    slot_grad = gradient_windows[0, 0, 0]
    slot_illum = illumination_windows[0, 0, 0]
    owners = window_owners[0, 0, 0]
    patches = window_patches[0, 0, 0]
    slot_count, levels, patch_rows, patch_cols = slot_grad.shape
    tile_rows, tile_cols = velocity.shape[1], velocity.shape[2]
    per_tile = tile_rows // patch_rows
    tiles = size_x * size_y
    cell_count = levels * patch_rows * patch_cols
    h = HALO
    ext_rows = tile_rows + 2 * h
    ext_cols = tile_cols + 2 * h

    owner_x = owners // size_y
    owner_y = owners % size_y
    rel_row = (((owner_x - me_x) % size_x) * size_y + (owner_y - me_y) % size_y) * per_tile + patches
    onehot = (rel_row[None, :] == jnp.arange(tiles * per_tile, dtype=jnp.int32)[:, None]).astype(
        jnp.bfloat16
    )
    both = jnp.concatenate(
        [slot_grad.reshape(slot_count, cell_count), slot_illum.reshape(slot_count, cell_count)],
        axis=1,
    )
    table = jnp.dot(onehot, both, preferred_element_type=jnp.float32)
    model = table.reshape(size_x, size_y, per_tile, 2, levels, patch_rows, patch_cols)
    model = model.transpose(3, 4, 0, 2, 5, 1, 6).reshape(
        2, levels, size_x * tile_rows, size_y * tile_cols
    )
    model = jnp.concatenate([model[:, :, -h:], model, model[:, :, :h]], axis=2)
    model = jnp.concatenate([model[:, :, :, -h:], model, model[:, :, :, :h]], axis=3)
    ext = jnp.stack(
        [
            jnp.stack(
                [
                    model[
                        :,
                        :,
                        tx * tile_rows : tx * tile_rows + ext_rows,
                        ty * tile_cols : ty * tile_cols + ext_cols,
                    ]
                    for ty in range(size_y)
                ]
            )
            for tx in range(size_x)
        ]
    )
    flat = ext.reshape(size_x, size_y, -1, 128)

    part = flat[0]
    for step in range(1, size_x):
        part = part + shifted(flat[step], "gx", size_x, step)
    total = part[0]
    for step in range(1, size_y):
        total = total + shifted(part[step], "gy", size_y, step)
    mine = total
    for step in range(1, size_g):
        total = total + shifted(mine, "group", size_g, step)

    sums = total.reshape(2, levels, ext_rows, ext_cols)
    pos_x = me_x * tile_rows - h + jnp.arange(ext_rows)
    pos_y = me_y * tile_cols - h + jnp.arange(ext_cols)
    inside = ((pos_x >= 0) & (pos_x < size_x * tile_rows))[:, None] & (
        (pos_y >= 0) & (pos_y < size_y * tile_cols)
    )[None, :]
    field_now = jnp.where(inside, sums[0] / (sums[1] + damping), 0.0)
    for sweep_index in range(SWEEPS):
        padded = jnp.pad(field_now, 1)
        beside = (
            (padded[1:-1, 2:, 1:-1] + padded[1:-1, :-2, 1:-1])
            + (padded[1:-1, 1:-1, 2:] + padded[1:-1, 1:-1, :-2])
            + (padded[2:, 1:-1, 1:-1] + padded[:-2, 1:-1, 1:-1])
        )
        field_now = jnp.where(inside, field_now + smooth_rate * (beside - 6.0 * field_now), 0.0)
    updated_model = velocity - step_length * field_now[:, h : h + tile_rows, h : h + tile_cols]

    tile_table = (
        updated_model.reshape(levels, per_tile, patch_rows, tile_cols)
        .transpose(1, 0, 2, 3)
        .reshape(per_tile, cell_count)
        .astype(jnp.bfloat16)
    )
    along_y = jnp.stack(
        [tile_table] + [shifted(tile_table, "gy", size_y, step) for step in range(1, size_y)]
    )
    along_x = jnp.stack(
        [along_y] + [shifted(along_y, "gx", size_x, step) for step in range(1, size_x)]
    )
    whole = along_x.reshape(tiles * per_tile, cell_count)
    back_row = (
        ((me_x - owner_x) % size_x) * size_y + (me_y - owner_y) % size_y
    ) * per_tile + patches
    pick = (back_row[:, None] == jnp.arange(tiles * per_tile, dtype=jnp.int32)[None, :]).astype(
        jnp.bfloat16
    )
    returned = jnp.dot(pick, whole, preferred_element_type=jnp.float32).astype(jnp.bfloat16)
    returned_windows = returned.reshape((1, 1, 1, slot_count, levels, patch_rows, patch_cols))
    return (updated_model, returned_windows)


def solution(mesh):
    return jax.shard_map(
        local,
        mesh=mesh,
        in_specs=(
            P("group", "gx", "gy", None, None, None, None),
            P("group", "gx", "gy", None, None, None, None),
            P("group", "gx", "gy", None),
            P("group", "gx", "gy", None),
            P(None, "gx", "gy"),
        ),
        out_specs=(P(None, "gx", "gy"), P("group", "gx", "gy", None, None, None, None)),
        check_vma=False,
    )
```

```python
import jax
import jax.numpy as jnp
from jax import lax
from jax.sharding import PartitionSpec as P

SWEEPS = 4
HALO = SWEEPS


damping = 10.0
smooth_rate = 0.12
step_length = 24.0


def shifted(value, axis, count, step):
    return lax.ppermute(value, axis, [(s, (s + step) % count) for s in range(count)])


def local(gradient_windows, illumination_windows, window_owners, window_patches, velocity):
    size_x = lax.axis_size("gx")
    size_y = lax.axis_size("gy")
    size_g = lax.axis_size("group")
    me_x = lax.axis_index("gx")
    me_y = lax.axis_index("gy")
    slot_grad = gradient_windows[0, 0, 0]
    slot_illum = illumination_windows[0, 0, 0]
    owners = window_owners[0, 0, 0]
    patches = window_patches[0, 0, 0]
    slot_count, levels, patch_rows, patch_cols = slot_grad.shape
    tile_rows, tile_cols = velocity.shape[1], velocity.shape[2]
    per_tile = tile_rows // patch_rows
    tiles = size_x * size_y
    cell_count = levels * patch_rows * patch_cols
    h = HALO
    ext_rows = tile_rows + 2 * h
    ext_cols = tile_cols + 2 * h

    me_g = lax.axis_index("group")
    quantities = jnp.stack(
        [slot_grad.reshape(slot_count, cell_count), slot_illum.reshape(slot_count, cell_count)]
    )
    kept = lax.dynamic_index_in_dim(quantities, me_g, 0, keepdims=False)
    given = lax.dynamic_index_in_dim(quantities, 1 - me_g, 0, keepdims=False)
    places = jnp.stack([owners, patches])
    taken = shifted(given, "group", size_g, 1)
    taken_places = shifted(places, "group", size_g, 1)
    rows_in = jnp.concatenate([kept, taken], axis=0)
    all_owners = jnp.concatenate([owners, taken_places[0]])
    all_patches = jnp.concatenate([patches, taken_places[1]])

    halo_patches = h // patch_rows
    ext_patches = per_tile + 2 * halo_patches
    rel_x = (all_owners // size_y - me_x) % size_x
    rel_y = (all_owners % size_y - me_y) % size_y
    own_row = (rel_x * size_y + rel_y) * ext_patches + all_patches + halo_patches
    next_row = jnp.where(
        all_patches >= per_tile - halo_patches,
        (((rel_x + 1) % size_x) * size_y + rel_y) * ext_patches
        + all_patches
        - (per_tile - halo_patches),
        -1,
    )
    prev_row = jnp.where(
        all_patches < halo_patches,
        (((rel_x - 1) % size_x) * size_y + rel_y) * ext_patches
        + all_patches
        + per_tile
        + halo_patches,
        -1,
    )
    row_ids = jnp.arange(tiles * ext_patches, dtype=jnp.int32)[:, None]
    onehot = (
        (own_row[None, :] == row_ids) | (next_row[None, :] == row_ids) | (prev_row[None, :] == row_ids)
    ).astype(jnp.bfloat16)
    table = jnp.dot(onehot, rows_in, preferred_element_type=jnp.float32)
    table = table.reshape(size_x, size_y, ext_patches, levels, patch_rows, patch_cols)
    left = jnp.roll(table, 1, axis=1)[..., patch_cols - h :]
    right = jnp.roll(table, -1, axis=1)[..., :h]
    strips = jnp.concatenate([left, right], axis=-1)
    flat = jnp.concatenate(
        [table.reshape(size_x, size_y, -1), strips.reshape(size_x, size_y, -1)], axis=2
    ).reshape(size_x, size_y, -1, 128)

    part = flat[0]
    for step in range(1, size_x):
        part = part + shifted(flat[step], "gx", size_x, step)
    total = part[0]
    for step in range(1, size_y):
        total = total + shifted(part[step], "gy", size_y, step)
    other = shifted(total, "group", size_g, 1)
    is_grad = me_g == 0
    grad_flat = jnp.where(is_grad, total, other).reshape(-1)
    illum_flat = jnp.where(is_grad, other, total).reshape(-1)

    def unpack(values):
        main_size = ext_patches * levels * patch_rows * patch_cols
        main = values[:main_size].reshape(ext_patches, levels, patch_rows, patch_cols)
        sides = values[main_size:].reshape(ext_patches, levels, patch_rows, 2 * h)
        whole_rows = jnp.concatenate([sides[..., :h], main, sides[..., h:]], axis=-1)
        return whole_rows.transpose(1, 0, 2, 3).reshape(levels, ext_rows, ext_cols)

    grad_ext = unpack(grad_flat)
    illum_ext = unpack(illum_flat)
    pos_x = me_x * tile_rows - h + jnp.arange(ext_rows)
    pos_y = me_y * tile_cols - h + jnp.arange(ext_cols)
    inside = ((pos_x >= 0) & (pos_x < size_x * tile_rows))[:, None] & (
        (pos_y >= 0) & (pos_y < size_y * tile_cols)
    )[None, :]
    field_now = jnp.where(inside, grad_ext / (illum_ext + damping), 0.0)
    for sweep_index in range(SWEEPS):
        padded = jnp.pad(field_now, 1)
        beside = (
            (padded[1:-1, 2:, 1:-1] + padded[1:-1, :-2, 1:-1])
            + (padded[1:-1, 1:-1, 2:] + padded[1:-1, 1:-1, :-2])
            + (padded[2:, 1:-1, 1:-1] + padded[:-2, 1:-1, 1:-1])
        )
        field_now = jnp.where(inside, field_now + smooth_rate * (beside - 6.0 * field_now), 0.0)
    updated_model = velocity - step_length * field_now[:, h : h + tile_rows, h : h + tile_cols]

    tile_table = (
        updated_model.reshape(levels, per_tile, patch_rows, tile_cols)
        .transpose(1, 0, 2, 3)
        .reshape(per_tile, cell_count)
        .astype(jnp.bfloat16)
    )
    along_y = jnp.stack(
        [tile_table] + [shifted(tile_table, "gy", size_y, step) for step in range(1, size_y)]
    )
    along_x = jnp.stack(
        [along_y] + [shifted(along_y, "gx", size_x, step) for step in range(1, size_x)]
    )
    whole = along_x.reshape(tiles * per_tile, cell_count)
    owner_x = owners // size_y
    owner_y = owners % size_y
    back_row = (
        ((me_x - owner_x) % size_x) * size_y + (me_y - owner_y) % size_y
    ) * per_tile + patches
    pick = (back_row[:, None] == jnp.arange(tiles * per_tile, dtype=jnp.int32)[None, :]).astype(
        jnp.bfloat16
    )
    returned = jnp.dot(pick, whole, preferred_element_type=jnp.float32).astype(jnp.bfloat16)
    returned_windows = returned.reshape((1, 1, 1, slot_count, levels, patch_rows, patch_cols))
    return (updated_model, returned_windows)


def solution(mesh):
    return jax.shard_map(
        local,
        mesh=mesh,
        in_specs=(
            P("group", "gx", "gy", None, None, None, None),
            P("group", "gx", "gy", None, None, None, None),
            P("group", "gx", "gy", None),
            P("group", "gx", "gy", None),
            P(None, "gx", "gy"),
        ),
        out_specs=(P(None, "gx", "gy"), P("group", "gx", "gy", None, None, None, None)),
        check_vma=False,
    )
```

```python
import jax
import jax.numpy as jnp
from jax import lax
from jax.sharding import PartitionSpec as P

SWEEPS = 4
HALO = SWEEPS


damping = 10.0
smooth_rate = 0.12
step_length = 24.0


def shifted(value, axis, count, step):
    return lax.ppermute(value, axis, [(s, (s + step) % count) for s in range(count)])


def local(gradient_windows, illumination_windows, window_owners, window_patches, velocity):
    size_x = lax.axis_size("gx")
    size_y = lax.axis_size("gy")
    size_g = lax.axis_size("group")
    me_x = lax.axis_index("gx")
    me_y = lax.axis_index("gy")
    slot_grad = gradient_windows[0, 0, 0]
    slot_illum = illumination_windows[0, 0, 0]
    owners = window_owners[0, 0, 0]
    patches = window_patches[0, 0, 0]
    slot_count, levels, patch_rows, patch_cols = slot_grad.shape
    tile_rows, tile_cols = velocity.shape[1], velocity.shape[2]
    per_tile = tile_rows // patch_rows
    tiles = size_x * size_y
    cell_count = levels * patch_rows * patch_cols
    h = HALO
    ext_rows = tile_rows + 2 * h
    ext_cols = tile_cols + 2 * h

    me_g = lax.axis_index("group")
    quantities = jnp.stack(
        [slot_grad.reshape(slot_count, cell_count), slot_illum.reshape(slot_count, cell_count)]
    )
    kept = lax.dynamic_index_in_dim(quantities, me_g, 0, keepdims=False)
    given = lax.dynamic_index_in_dim(quantities, 1 - me_g, 0, keepdims=False)
    places = jnp.stack([owners, patches])
    taken = shifted(given, "group", size_g, 1)
    taken_places = shifted(places, "group", size_g, 1)
    rows_in = jnp.concatenate([kept, taken], axis=0)
    all_owners = jnp.concatenate([owners, taken_places[0]])
    all_patches = jnp.concatenate([patches, taken_places[1]])

    halo_patches = h // patch_rows
    ext_patches = per_tile + 2 * halo_patches
    rel_x = (all_owners // size_y - me_x) % size_x
    rel_y = (all_owners % size_y - me_y) % size_y
    own_row = (rel_x * size_y + rel_y) * ext_patches + all_patches + halo_patches
    next_row = jnp.where(
        all_patches >= per_tile - halo_patches,
        (((rel_x + 1) % size_x) * size_y + rel_y) * ext_patches
        + all_patches
        - (per_tile - halo_patches),
        -1,
    )
    prev_row = jnp.where(
        all_patches < halo_patches,
        (((rel_x - 1) % size_x) * size_y + rel_y) * ext_patches
        + all_patches
        + per_tile
        + halo_patches,
        -1,
    )
    row_ids = jnp.arange(tiles * ext_patches, dtype=jnp.int32)[:, None]
    onehot = (
        (own_row[None, :] == row_ids) | (next_row[None, :] == row_ids) | (prev_row[None, :] == row_ids)
    ).astype(jnp.bfloat16)
    table = jnp.dot(onehot, rows_in, preferred_element_type=jnp.float32)
    flat = table.reshape(size_x, size_y * ext_patches, cell_count)

    part = flat[0]
    for step in range(1, size_x):
        part = part + shifted(flat[step], "gx", size_x, step)
    part = part.reshape(size_y, ext_patches, levels, patch_rows, patch_cols)
    left = jnp.roll(part, 1, axis=0)[..., patch_cols - h :]
    right = jnp.roll(part, -1, axis=0)[..., :h]
    strips = jnp.concatenate([left, right], axis=-1)
    packed = jnp.concatenate(
        [part.reshape(size_y, -1), strips.reshape(size_y, -1)], axis=1
    ).reshape(size_y, -1, 128)
    total = packed[0]
    for step in range(1, size_y):
        total = total + shifted(packed[step], "gy", size_y, step)
    other = shifted(total, "group", size_g, 1)
    is_grad = me_g == 0
    grad_flat = jnp.where(is_grad, total, other).reshape(-1)
    illum_flat = jnp.where(is_grad, other, total).reshape(-1)

    def unpack(values):
        main_size = ext_patches * levels * patch_rows * patch_cols
        main = values[:main_size].reshape(ext_patches, levels, patch_rows, patch_cols)
        sides = values[main_size:].reshape(ext_patches, levels, patch_rows, 2 * h)
        whole_rows = jnp.concatenate([sides[..., :h], main, sides[..., h:]], axis=-1)
        return whole_rows.transpose(1, 0, 2, 3).reshape(levels, ext_rows, ext_cols)

    grad_ext = unpack(grad_flat)
    illum_ext = unpack(illum_flat)
    pos_x = me_x * tile_rows - h + jnp.arange(ext_rows)
    pos_y = me_y * tile_cols - h + jnp.arange(ext_cols)
    inside = ((pos_x >= 0) & (pos_x < size_x * tile_rows))[:, None] & (
        (pos_y >= 0) & (pos_y < size_y * tile_cols)
    )[None, :]
    field_now = jnp.where(inside, grad_ext / (illum_ext + damping), 0.0)
    for sweep_index in range(SWEEPS):
        padded = jnp.pad(field_now, 1)
        beside = (
            (padded[1:-1, 2:, 1:-1] + padded[1:-1, :-2, 1:-1])
            + (padded[1:-1, 1:-1, 2:] + padded[1:-1, 1:-1, :-2])
            + (padded[2:, 1:-1, 1:-1] + padded[:-2, 1:-1, 1:-1])
        )
        field_now = jnp.where(inside, field_now + smooth_rate * (beside - 6.0 * field_now), 0.0)
    updated_model = velocity - step_length * field_now[:, h : h + tile_rows, h : h + tile_cols]

    tile_table = (
        updated_model.reshape(levels, per_tile, patch_rows, tile_cols)
        .transpose(1, 0, 2, 3)
        .reshape(per_tile, cell_count)
        .astype(jnp.bfloat16)
    )
    along_y = jnp.stack(
        [tile_table] + [shifted(tile_table, "gy", size_y, step) for step in range(1, size_y)]
    )
    along_x = jnp.stack(
        [along_y] + [shifted(along_y, "gx", size_x, step) for step in range(1, size_x)]
    )
    whole = along_x.reshape(tiles * per_tile, cell_count)
    owner_x = owners // size_y
    owner_y = owners % size_y
    back_row = (
        ((me_x - owner_x) % size_x) * size_y + (me_y - owner_y) % size_y
    ) * per_tile + patches
    pick = (back_row[:, None] == jnp.arange(tiles * per_tile, dtype=jnp.int32)[None, :]).astype(
        jnp.bfloat16
    )
    returned = jnp.dot(pick, whole, preferred_element_type=jnp.float32).astype(jnp.bfloat16)
    returned_windows = returned.reshape((1, 1, 1, slot_count, levels, patch_rows, patch_cols))
    return (updated_model, returned_windows)


def solution(mesh):
    return jax.shard_map(
        local,
        mesh=mesh,
        in_specs=(
            P("group", "gx", "gy", None, None, None, None),
            P("group", "gx", "gy", None, None, None, None),
            P("group", "gx", "gy", None),
            P("group", "gx", "gy", None),
            P(None, "gx", "gy"),
        ),
        out_specs=(P(None, "gx", "gy"), P("group", "gx", "gy", None, None, None, None)),
        check_vma=False,
    )
```

```python
import jax
import jax.numpy as jnp
from jax import lax
from jax.sharding import PartitionSpec as P

SWEEPS = 4
HALO = SWEEPS


damping = 10.0
smooth_rate = 0.12
step_length = 24.0


def shifted(value, axis, count, step):
    return lax.ppermute(value, axis, [(s, (s + step) % count) for s in range(count)])


def local(gradient_windows, illumination_windows, window_owners, window_patches, velocity):
    size_x = lax.axis_size("gx")
    size_y = lax.axis_size("gy")
    size_g = lax.axis_size("group")
    me_x = lax.axis_index("gx")
    me_y = lax.axis_index("gy")
    slot_grad = gradient_windows[0, 0, 0]
    slot_illum = illumination_windows[0, 0, 0]
    owners = window_owners[0, 0, 0]
    patches = window_patches[0, 0, 0]
    slot_count, levels, patch_rows, patch_cols = slot_grad.shape
    tile_rows, tile_cols = velocity.shape[1], velocity.shape[2]
    per_tile = tile_rows // patch_rows
    tiles = size_x * size_y
    cell_count = levels * patch_rows * patch_cols
    h = HALO
    ext_rows = tile_rows + 2 * h
    ext_cols = tile_cols + 2 * h

    me_g = lax.axis_index("group")
    is_grad = me_g == 0
    kept = jnp.where(is_grad, slot_grad, slot_illum)
    given = jnp.where(is_grad, slot_illum, slot_grad)
    places = jnp.stack([owners, patches])
    taken = shifted(given, "group", size_g, 1)
    taken_places = shifted(places, "group", size_g, 1)
    rows_in = jnp.concatenate([kept, taken], axis=0)
    all_owners = jnp.concatenate([owners, taken_places[0]])
    all_patches = jnp.concatenate([patches, taken_places[1]])

    halo_patches = h // patch_rows
    ext_patches = per_tile + 2 * halo_patches
    rel_x = (all_owners // size_y - me_x) % size_x
    rel_y = (all_owners % size_y - me_y) % size_y
    own_row = (rel_x * size_y + rel_y) * ext_patches + all_patches + halo_patches
    next_row = jnp.where(
        all_patches >= per_tile - halo_patches,
        (((rel_x + 1) % size_x) * size_y + rel_y) * ext_patches
        + all_patches
        - (per_tile - halo_patches),
        -1,
    )
    prev_row = jnp.where(
        all_patches < halo_patches,
        (((rel_x - 1) % size_x) * size_y + rel_y) * ext_patches
        + all_patches
        + per_tile
        + halo_patches,
        -1,
    )
    row_ids = jnp.arange(tiles * ext_patches, dtype=jnp.int32)[:, None]
    onehot = (
        (own_row[None, :] == row_ids) | (next_row[None, :] == row_ids) | (prev_row[None, :] == row_ids)
    ).astype(jnp.bfloat16)
    table = jnp.einsum("rw,wlpc->rlpc", onehot, rows_in, preferred_element_type=jnp.float32)
    flat = table.reshape(size_x, size_y * ext_patches, levels, patch_rows, patch_cols)

    part = flat[0]
    for step in range(1, size_x):
        part = part + shifted(flat[step], "gx", size_x, step)
    part = part.reshape(size_y, ext_patches, levels, patch_rows, patch_cols)
    left = jnp.roll(part, 1, axis=0)[..., patch_cols - h :]
    right = jnp.roll(part, -1, axis=0)[..., :h]
    strips = jnp.concatenate([left, right], axis=-1)
    packed = jnp.concatenate(
        [part.reshape(size_y, -1), strips.reshape(size_y, -1)], axis=1
    ).reshape(size_y, -1, 128)
    total = packed[0]
    for step in range(1, size_y):
        total = total + shifted(packed[step], "gy", size_y, step)
    other = shifted(total, "group", size_g, 1)
    grad_flat = jnp.where(is_grad, total, other).reshape(-1)
    illum_flat = jnp.where(is_grad, other, total).reshape(-1)

    def unpack(values):
        main_size = ext_patches * levels * patch_rows * patch_cols
        main = values[:main_size].reshape(ext_patches, levels, patch_rows, patch_cols)
        sides = values[main_size:].reshape(ext_patches, levels, patch_rows, 2 * h)
        whole_rows = jnp.concatenate([sides[..., :h], main, sides[..., h:]], axis=-1)
        return whole_rows.transpose(1, 0, 2, 3).reshape(levels, ext_rows, ext_cols)

    grad_ext = unpack(grad_flat)
    illum_ext = unpack(illum_flat)
    pos_x = me_x * tile_rows - h + jnp.arange(ext_rows)
    pos_y = me_y * tile_cols - h + jnp.arange(ext_cols)
    inside = ((pos_x >= 0) & (pos_x < size_x * tile_rows))[:, None] & (
        (pos_y >= 0) & (pos_y < size_y * tile_cols)
    )[None, :]
    field_now = jnp.where(inside, grad_ext / (illum_ext + damping), 0.0)
    for sweep_index in range(SWEEPS):
        padded = jnp.pad(field_now, 1)
        beside = (
            (padded[1:-1, 2:, 1:-1] + padded[1:-1, :-2, 1:-1])
            + (padded[1:-1, 1:-1, 2:] + padded[1:-1, 1:-1, :-2])
            + (padded[2:, 1:-1, 1:-1] + padded[:-2, 1:-1, 1:-1])
        )
        field_now = jnp.where(inside, field_now + smooth_rate * (beside - 6.0 * field_now), 0.0)
    updated_model = velocity - step_length * field_now[:, h : h + tile_rows, h : h + tile_cols]

    tile_table = (
        updated_model.reshape(levels, per_tile, patch_rows, tile_cols)
        .transpose(1, 0, 2, 3)
        .astype(jnp.bfloat16)
    )
    along_y = jnp.stack(
        [tile_table] + [shifted(tile_table, "gy", size_y, step) for step in range(1, size_y)]
    )
    along_x = jnp.stack(
        [along_y] + [shifted(along_y, "gx", size_x, step) for step in range(1, size_x)]
    )
    whole = along_x.reshape(tiles * per_tile, levels, patch_rows, patch_cols)
    owner_x = owners // size_y
    owner_y = owners % size_y
    back_row = (
        ((me_x - owner_x) % size_x) * size_y + (me_y - owner_y) % size_y
    ) * per_tile + patches
    pick = (back_row[:, None] == jnp.arange(tiles * per_tile, dtype=jnp.int32)[None, :]).astype(
        jnp.bfloat16
    )
    returned = jnp.einsum("wr,rlpc->wlpc", pick, whole, preferred_element_type=jnp.float32).astype(
        jnp.bfloat16
    )
    returned_windows = returned.reshape((1, 1, 1, slot_count, levels, patch_rows, patch_cols))
    return (updated_model, returned_windows)


def solution(mesh):
    return jax.shard_map(
        local,
        mesh=mesh,
        in_specs=(
            P("group", "gx", "gy", None, None, None, None),
            P("group", "gx", "gy", None, None, None, None),
            P("group", "gx", "gy", None),
            P("group", "gx", "gy", None),
            P(None, "gx", "gy"),
        ),
        out_specs=(P(None, "gx", "gy"), P("group", "gx", "gy", None, None, None, None)),
        check_vma=False,
    )
```

```python
import jax
import jax.numpy as jnp
from jax import lax
from jax.sharding import PartitionSpec as P

SWEEPS = 4
HALO = SWEEPS


damping = 10.0
smooth_rate = 0.12
step_length = 24.0


def shifted(value, axis, count, step):
    return lax.ppermute(value, axis, [(s, (s + step) % count) for s in range(count)])


def local(gradient_windows, illumination_windows, window_owners, window_patches, velocity):
    size_x = lax.axis_size("gx")
    size_y = lax.axis_size("gy")
    size_g = lax.axis_size("group")
    me_x = lax.axis_index("gx")
    me_y = lax.axis_index("gy")
    slot_grad = gradient_windows[0, 0, 0]
    slot_illum = illumination_windows[0, 0, 0]
    owners = window_owners[0, 0, 0]
    patches = window_patches[0, 0, 0]
    slot_count, levels, patch_rows, patch_cols = slot_grad.shape
    tile_rows, tile_cols = velocity.shape[1], velocity.shape[2]
    per_tile = tile_rows // patch_rows
    tiles = size_x * size_y
    cell_count = levels * patch_rows * patch_cols
    h = HALO
    ext_rows = tile_rows + 2 * h
    ext_cols = tile_cols + 2 * h

    me_g = lax.axis_index("group")
    is_grad = me_g == 0
    kept = jnp.where(is_grad, slot_grad, slot_illum)
    taken = lax.ppermute(slot_illum, "group", [(0, 1)]) + lax.ppermute(slot_grad, "group", [(1, 0)])
    places = jnp.stack([owners, patches])
    taken_places = shifted(places, "group", size_g, 1)
    rows_in = jnp.concatenate([kept, taken], axis=0)
    all_owners = jnp.concatenate([owners, taken_places[0]])
    all_patches = jnp.concatenate([patches, taken_places[1]])

    halo_patches = h // patch_rows
    ext_patches = per_tile + 2 * halo_patches
    rel_x = (all_owners // size_y - me_x) % size_x
    rel_y = (all_owners % size_y - me_y) % size_y
    own_row = (rel_x * size_y + rel_y) * ext_patches + all_patches + halo_patches
    next_row = jnp.where(
        all_patches >= per_tile - halo_patches,
        (((rel_x + 1) % size_x) * size_y + rel_y) * ext_patches
        + all_patches
        - (per_tile - halo_patches),
        -1,
    )
    prev_row = jnp.where(
        all_patches < halo_patches,
        (((rel_x - 1) % size_x) * size_y + rel_y) * ext_patches
        + all_patches
        + per_tile
        + halo_patches,
        -1,
    )
    row_ids = jnp.arange(tiles * ext_patches, dtype=jnp.int32)[:, None]
    onehot = (
        (own_row[None, :] == row_ids) | (next_row[None, :] == row_ids) | (prev_row[None, :] == row_ids)
    ).astype(jnp.bfloat16)
    table = jnp.einsum("rw,wlpc->rlpc", onehot, rows_in, preferred_element_type=jnp.float32)
    flat = table.reshape(size_x, size_y * ext_patches, levels, patch_rows, patch_cols)

    part = flat[0]
    for step in range(1, size_x):
        part = part + shifted(flat[step], "gx", size_x, step)
    part = part.reshape(size_y, ext_patches, levels, patch_rows, patch_cols)
    left = jnp.roll(part, 1, axis=0)[..., patch_cols - h :]
    right = jnp.roll(part, -1, axis=0)[..., :h]
    strips = jnp.concatenate([left, right], axis=-1)
    packed = jnp.concatenate(
        [part.reshape(size_y, -1), strips.reshape(size_y, -1)], axis=1
    ).reshape(size_y, -1, 128)
    total = packed[0]
    for step in range(1, size_y):
        total = total + shifted(packed[step], "gy", size_y, step)
    other = shifted(total, "group", size_g, 1)
    grad_flat = jnp.where(is_grad, total, other).reshape(-1)
    illum_flat = jnp.where(is_grad, other, total).reshape(-1)

    def unpack(values):
        main_size = ext_patches * levels * patch_rows * patch_cols
        main = values[:main_size].reshape(ext_patches, levels, patch_rows, patch_cols)
        sides = values[main_size:].reshape(ext_patches, levels, patch_rows, 2 * h)
        whole_rows = jnp.concatenate([sides[..., :h], main, sides[..., h:]], axis=-1)
        return whole_rows.transpose(1, 0, 2, 3).reshape(levels, ext_rows, ext_cols)

    grad_ext = unpack(grad_flat)
    illum_ext = unpack(illum_flat)
    pos_x = me_x * tile_rows - h + jnp.arange(ext_rows)
    pos_y = me_y * tile_cols - h + jnp.arange(ext_cols)
    inside = ((pos_x >= 0) & (pos_x < size_x * tile_rows))[:, None] & (
        (pos_y >= 0) & (pos_y < size_y * tile_cols)
    )[None, :]
    field_now = jnp.where(inside, grad_ext / (illum_ext + damping), 0.0)
    for sweep_index in range(SWEEPS):
        padded = jnp.pad(field_now, 1)
        beside = (
            (padded[1:-1, 2:, 1:-1] + padded[1:-1, :-2, 1:-1])
            + (padded[1:-1, 1:-1, 2:] + padded[1:-1, 1:-1, :-2])
            + (padded[2:, 1:-1, 1:-1] + padded[:-2, 1:-1, 1:-1])
        )
        field_now = jnp.where(inside, field_now + smooth_rate * (beside - 6.0 * field_now), 0.0)
    updated_model = velocity - step_length * field_now[:, h : h + tile_rows, h : h + tile_cols]

    tile_table = (
        updated_model.reshape(levels, per_tile, patch_rows, tile_cols)
        .transpose(1, 0, 2, 3)
        .astype(jnp.bfloat16)
    )
    along_y = jnp.stack(
        [tile_table] + [shifted(tile_table, "gy", size_y, step) for step in range(1, size_y)]
    )
    along_x = jnp.stack(
        [along_y] + [shifted(along_y, "gx", size_x, step) for step in range(1, size_x)]
    )
    whole = along_x.reshape(tiles * per_tile, levels, patch_rows, patch_cols)
    owner_x = owners // size_y
    owner_y = owners % size_y
    back_row = (
        ((me_x - owner_x) % size_x) * size_y + (me_y - owner_y) % size_y
    ) * per_tile + patches
    pick = (back_row[:, None] == jnp.arange(tiles * per_tile, dtype=jnp.int32)[None, :]).astype(
        jnp.bfloat16
    )
    returned = jnp.einsum("wr,rlpc->wlpc", pick, whole, preferred_element_type=jnp.float32).astype(
        jnp.bfloat16
    )
    returned_windows = returned.reshape((1, 1, 1, slot_count, levels, patch_rows, patch_cols))
    return (updated_model, returned_windows)


def solution(mesh):
    return jax.shard_map(
        local,
        mesh=mesh,
        in_specs=(
            P("group", "gx", "gy", None, None, None, None),
            P("group", "gx", "gy", None, None, None, None),
            P("group", "gx", "gy", None),
            P("group", "gx", "gy", None),
            P(None, "gx", "gy"),
        ),
        out_specs=(P(None, "gx", "gy"), P("group", "gx", "gy", None, None, None, None)),
        check_vma=False,
    )
```

```python
import jax
import jax.numpy as jnp
from jax import lax
from jax.sharding import PartitionSpec as P

SWEEPS = 4
HALO = SWEEPS


damping = 10.0
smooth_rate = 0.12
step_length = 24.0


def shifted(value, axis, count, step):
    return lax.ppermute(value, axis, [(s, (s + step) % count) for s in range(count)])


def local(gradient_windows, illumination_windows, window_owners, window_patches, velocity):
    size_x = lax.axis_size("gx")
    size_y = lax.axis_size("gy")
    size_g = lax.axis_size("group")
    me_x = lax.axis_index("gx")
    me_y = lax.axis_index("gy")
    slot_grad = gradient_windows[0, 0, 0]
    slot_illum = illumination_windows[0, 0, 0]
    owners = window_owners[0, 0, 0]
    patches = window_patches[0, 0, 0]
    slot_count, levels, patch_rows, patch_cols = slot_grad.shape
    tile_rows, tile_cols = velocity.shape[1], velocity.shape[2]
    per_tile = tile_rows // patch_rows
    tiles = size_x * size_y
    cell_count = levels * patch_rows * patch_cols
    h = HALO
    ext_rows = tile_rows + 2 * h

    me_g = lax.axis_index("group")
    is_grad = me_g == 0
    kept = jnp.where(is_grad, slot_grad, slot_illum)
    given = jnp.where(is_grad, slot_illum, slot_grad)
    places = jnp.stack([owners, patches])
    taken = shifted(given, "group", size_g, 1)
    taken_places = shifted(places, "group", size_g, 1)
    rows_in = jnp.concatenate([kept, taken], axis=0)
    all_owners = jnp.concatenate([owners, taken_places[0]])
    all_patches = jnp.concatenate([patches, taken_places[1]])

    halo_patches = h // patch_rows
    ext_patches = per_tile + 2 * halo_patches
    rel_x = (all_owners // size_y - me_x) % size_x
    abs_y = all_owners % size_y
    own_row = (rel_x * size_y + abs_y) * ext_patches + all_patches + halo_patches
    next_row = jnp.where(
        all_patches >= per_tile - halo_patches,
        (((rel_x + 1) % size_x) * size_y + abs_y) * ext_patches
        + all_patches
        - (per_tile - halo_patches),
        -1,
    )
    prev_row = jnp.where(
        all_patches < halo_patches,
        (((rel_x - 1) % size_x) * size_y + abs_y) * ext_patches
        + all_patches
        + per_tile
        + halo_patches,
        -1,
    )
    row_ids = jnp.arange(tiles * ext_patches, dtype=jnp.int32)[:, None]
    onehot = (
        (own_row[None, :] == row_ids) | (next_row[None, :] == row_ids) | (prev_row[None, :] == row_ids)
    ).astype(jnp.bfloat16)
    table = jnp.einsum("rw,wlpc->rlpc", onehot, rows_in, preferred_element_type=jnp.float32)
    flat = table.reshape(size_x, size_y * ext_patches, levels, patch_rows, patch_cols)

    velocity_seen = jnp.stack(
        [velocity] + [shifted(velocity, "gy", size_y, step) for step in range(1, size_y)]
    )
    velocity_row = jnp.take(velocity_seen, (me_y - jnp.arange(size_y)) % size_y, axis=0)
    velocity_row = velocity_row.transpose(1, 2, 0, 3).reshape(levels, tile_rows, size_y * tile_cols)

    part = flat[0]
    for step in range(1, size_x):
        part = part + shifted(flat[step], "gx", size_x, step)
    row_sums = part
    for step in range(1, size_y):
        row_sums = row_sums + shifted(part, "gy", size_y, step)
    other = shifted(row_sums, "group", size_g, 1)

    def unpack(values):
        return values.reshape(size_y, ext_patches, levels, patch_rows, patch_cols).transpose(
            2, 1, 3, 0, 4
        ).reshape(levels, ext_rows, size_y * tile_cols)

    grad_ext = unpack(jnp.where(is_grad, row_sums, other))
    illum_ext = unpack(jnp.where(is_grad, other, row_sums))
    pos_x = me_x * tile_rows - h + jnp.arange(ext_rows)
    inside = ((pos_x >= 0) & (pos_x < size_x * tile_rows))[:, None]
    field_now = jnp.where(inside, grad_ext / (illum_ext + damping), 0.0)
    for sweep_index in range(SWEEPS):
        padded = jnp.pad(field_now, 1)
        beside = (
            (padded[1:-1, 2:, 1:-1] + padded[1:-1, :-2, 1:-1])
            + (padded[1:-1, 1:-1, 2:] + padded[1:-1, 1:-1, :-2])
            + (padded[2:, 1:-1, 1:-1] + padded[:-2, 1:-1, 1:-1])
        )
        field_now = jnp.where(inside, field_now + smooth_rate * (beside - 6.0 * field_now), 0.0)
    updated_row = velocity_row - step_length * field_now[:, h : h + tile_rows, :]
    updated_model = lax.dynamic_slice_in_dim(updated_row, me_y * tile_cols, tile_cols, axis=2)

    row_table = (
        updated_row.reshape(levels, per_tile, patch_rows, size_y, tile_cols)
        .transpose(3, 1, 0, 2, 4)
        .astype(jnp.bfloat16)
    )
    along_x = jnp.stack(
        [row_table] + [shifted(row_table, "gx", size_x, step) for step in range(1, size_x)]
    )
    whole = along_x.reshape(tiles * per_tile, levels, patch_rows, patch_cols)
    owner_x = owners // size_y
    owner_y = owners % size_y
    back_row = (((me_x - owner_x) % size_x) * size_y + owner_y) * per_tile + patches
    pick = (back_row[:, None] == jnp.arange(tiles * per_tile, dtype=jnp.int32)[None, :]).astype(
        jnp.bfloat16
    )
    returned = jnp.einsum("wr,rlpc->wlpc", pick, whole, preferred_element_type=jnp.float32).astype(
        jnp.bfloat16
    )
    returned_windows = returned.reshape((1, 1, 1, slot_count, levels, patch_rows, patch_cols))
    return (updated_model, returned_windows)


def solution(mesh):
    return jax.shard_map(
        local,
        mesh=mesh,
        in_specs=(
            P("group", "gx", "gy", None, None, None, None),
            P("group", "gx", "gy", None, None, None, None),
            P("group", "gx", "gy", None),
            P("group", "gx", "gy", None),
            P(None, "gx", "gy"),
        ),
        out_specs=(P(None, "gx", "gy"), P("group", "gx", "gy", None, None, None, None)),
        check_vma=False,
    )
```

```python
import jax
import jax.numpy as jnp
from jax import lax
from jax.sharding import PartitionSpec as P

SWEEPS = 4
HALO = SWEEPS


damping = 10.0
smooth_rate = 0.12
step_length = 24.0


def shifted(value, axis, count, step):
    return lax.ppermute(value, axis, [(s, (s + step) % count) for s in range(count)])


def local(gradient_windows, illumination_windows, window_owners, window_patches, velocity):
    size_x = lax.axis_size("gx")
    size_y = lax.axis_size("gy")
    size_g = lax.axis_size("group")
    me_x = lax.axis_index("gx")
    me_y = lax.axis_index("gy")
    slot_grad = gradient_windows[0, 0, 0]
    slot_illum = illumination_windows[0, 0, 0]
    owners = window_owners[0, 0, 0]
    patches = window_patches[0, 0, 0]
    slot_count, levels, patch_rows, patch_cols = slot_grad.shape
    tile_rows, tile_cols = velocity.shape[1], velocity.shape[2]
    per_tile = tile_rows // patch_rows
    tiles = size_x * size_y
    cell_count = levels * patch_rows * patch_cols
    h = HALO
    ext_rows = tile_rows + 2 * h
    ext_cols = tile_cols + 2 * h

    me_g = lax.axis_index("group")
    is_grad = me_g == 0
    kept = jnp.where(is_grad, slot_grad, slot_illum)
    given = jnp.where(is_grad, slot_illum, slot_grad)
    places = jnp.stack([owners, patches])
    taken = shifted(given, "group", size_g, 1)
    taken_places = shifted(places, "group", size_g, 1)
    rows_in = jnp.concatenate([kept, taken], axis=0)
    all_owners = jnp.concatenate([owners, taken_places[0]])
    all_patches = jnp.concatenate([patches, taken_places[1]])

    halo_patches = h // patch_rows
    ext_patches = per_tile + 2 * halo_patches
    rel_x = (all_owners // size_y - me_x) % size_x
    rel_y = (all_owners % size_y - me_y) % size_y
    own_row = (rel_x * size_y + rel_y) * ext_patches + all_patches + halo_patches
    next_row = jnp.where(
        all_patches >= per_tile - halo_patches,
        (((rel_x + 1) % size_x) * size_y + rel_y) * ext_patches
        + all_patches
        - (per_tile - halo_patches),
        -1,
    )
    prev_row = jnp.where(
        all_patches < halo_patches,
        (((rel_x - 1) % size_x) * size_y + rel_y) * ext_patches
        + all_patches
        + per_tile
        + halo_patches,
        -1,
    )
    row_ids = jnp.arange(tiles * ext_patches, dtype=jnp.int32)[:, None]
    onehot = (
        (own_row[None, :] == row_ids) | (next_row[None, :] == row_ids) | (prev_row[None, :] == row_ids)
    ).astype(jnp.bfloat16)
    table = jnp.einsum("rw,wlpc->rlpc", onehot, rows_in, preferred_element_type=jnp.float32)
    flat = table.reshape(size_x, size_y * ext_patches, levels, patch_rows, patch_cols)

    part = flat[0]
    for step in range(1, size_x):
        part = part + shifted(flat[step], "gx", size_x, step)
    part = part.reshape(size_y, ext_patches, levels, patch_rows, patch_cols)
    left = jnp.roll(part, 1, axis=0)[..., patch_cols - h :]
    right = jnp.roll(part, -1, axis=0)[..., :h]
    strips = jnp.concatenate([left, right], axis=-1)
    packed = jnp.concatenate(
        [part.reshape(size_y, -1), strips.reshape(size_y, -1)], axis=1
    ).reshape(size_y, -1, 128)
    total = packed[0]
    for step in range(1, size_y):
        total = total + shifted(packed[step], "gy", size_y, step)
    other = shifted(total, "group", size_g, 1)
    grad_flat = jnp.where(is_grad, total, other).reshape(-1)
    illum_flat = jnp.where(is_grad, other, total).reshape(-1)

    def unpack(values):
        main_size = ext_patches * levels * patch_rows * patch_cols
        main = values[:main_size].reshape(ext_patches, levels, patch_rows, patch_cols)
        sides = values[main_size:].reshape(ext_patches, levels, patch_rows, 2 * h)
        whole_rows = jnp.concatenate([sides[..., :h], main, sides[..., h:]], axis=-1)
        return whole_rows.transpose(1, 0, 2, 3).reshape(levels, ext_rows, ext_cols)

    grad_ext = unpack(grad_flat)
    illum_ext = unpack(illum_flat)
    pos_x = me_x * tile_rows - h + jnp.arange(ext_rows)
    pos_y = me_y * tile_cols - h + jnp.arange(ext_cols)
    inside = ((pos_x >= 0) & (pos_x < size_x * tile_rows))[:, None] & (
        (pos_y >= 0) & (pos_y < size_y * tile_cols)
    )[None, :]
    field_now = jnp.where(inside, grad_ext / (illum_ext + damping), 0.0)
    for sweep_index in range(SWEEPS):
        padded = jnp.pad(field_now, 1)
        beside = (
            (padded[1:-1, 2:, 1:-1] + padded[1:-1, :-2, 1:-1])
            + (padded[1:-1, 1:-1, 2:] + padded[1:-1, 1:-1, :-2])
            + (padded[2:, 1:-1, 1:-1] + padded[:-2, 1:-1, 1:-1])
        )
        field_now = jnp.where(inside, field_now + smooth_rate * (beside - 6.0 * field_now), 0.0)
    updated_model = velocity - step_length * field_now[:, h : h + tile_rows, h : h + tile_cols]

    tile_table = (
        updated_model.reshape(levels, per_tile, patch_rows, tile_cols)
        .transpose(1, 0, 2, 3)
        .astype(jnp.bfloat16)
    )
    along_y = jnp.stack(
        [tile_table] + [shifted(tile_table, "gy", size_y, step) for step in range(1, size_y)]
    )
    along_x = jnp.stack(
        [along_y] + [shifted(along_y, "gx", size_x, step) for step in range(1, size_x)]
    )
    whole = along_x.reshape(tiles * per_tile, levels, patch_rows, patch_cols)
    owner_x = owners // size_y
    owner_y = owners % size_y
    back_row = (
        ((me_x - owner_x) % size_x) * size_y + (me_y - owner_y) % size_y
    ) * per_tile + patches
    rows_per_window = levels * patch_rows
    target = (
        back_row[:, None] * rows_per_window + jnp.arange(rows_per_window, dtype=jnp.int32)[None, :]
    ).reshape(-1)
    pick = (
        target[:, None] == jnp.arange(tiles * per_tile * rows_per_window, dtype=jnp.int32)[None, :]
    ).astype(jnp.bfloat16)
    returned = jnp.dot(
        pick, whole.reshape(-1, patch_cols), preferred_element_type=jnp.float32
    ).astype(jnp.bfloat16)
    returned_windows = returned.reshape((1, 1, 1, slot_count, levels, patch_rows, patch_cols))
    return (updated_model, returned_windows)


def solution(mesh):
    return jax.shard_map(
        local,
        mesh=mesh,
        in_specs=(
            P("group", "gx", "gy", None, None, None, None),
            P("group", "gx", "gy", None, None, None, None),
            P("group", "gx", "gy", None),
            P("group", "gx", "gy", None),
            P(None, "gx", "gy"),
        ),
        out_specs=(P(None, "gx", "gy"), P("group", "gx", "gy", None, None, None, None)),
        check_vma=False,
    )
```

```python
import jax
import jax.numpy as jnp
from jax import lax
from jax.sharding import PartitionSpec as P

SWEEPS = 4
HALO = SWEEPS


damping = 10.0
smooth_rate = 0.12
step_length = 24.0


def shifted(value, axis, count, step):
    return lax.ppermute(value, axis, [(s, (s + step) % count) for s in range(count)])


def local(gradient_windows, illumination_windows, window_owners, window_patches, velocity):
    size_x = lax.axis_size("gx")
    size_y = lax.axis_size("gy")
    size_g = lax.axis_size("group")
    me_x = lax.axis_index("gx")
    me_y = lax.axis_index("gy")
    slot_grad = gradient_windows[0, 0, 0]
    slot_illum = illumination_windows[0, 0, 0]
    owners = window_owners[0, 0, 0]
    patches = window_patches[0, 0, 0]
    slot_count, levels, patch_rows, patch_cols = slot_grad.shape
    tile_rows, tile_cols = velocity.shape[1], velocity.shape[2]
    per_tile = tile_rows // patch_rows
    tiles = size_x * size_y
    cell_count = levels * patch_rows * patch_cols
    h = HALO
    ext_rows = tile_rows + 2 * h
    ext_cols = tile_cols + 2 * h

    me_g = lax.axis_index("group")
    is_grad = me_g == 0
    kept = jnp.where(is_grad, slot_grad, slot_illum)
    given = jnp.where(is_grad, slot_illum, slot_grad)
    block_size = levels * patch_rows * patch_cols
    places = jnp.concatenate(
        [owners, patches, jnp.zeros((block_size - 2 * slot_count,), jnp.int32)]
    ).astype(jnp.bfloat16)
    sent = jnp.concatenate([given, places.reshape(1, levels, patch_rows, patch_cols)], axis=0)
    arrived = shifted(sent, "group", size_g, 1)
    taken = arrived[:slot_count]
    taken_places = arrived[slot_count].reshape(-1).astype(jnp.int32)
    rows_in = jnp.concatenate([kept, taken], axis=0)
    all_owners = jnp.concatenate([owners, taken_places[:slot_count]])
    all_patches = jnp.concatenate([patches, taken_places[slot_count : 2 * slot_count]])

    halo_patches = h // patch_rows
    ext_patches = per_tile + 2 * halo_patches
    rel_x = (all_owners // size_y - me_x) % size_x
    rel_y = (all_owners % size_y - me_y) % size_y
    own_row = (rel_x * size_y + rel_y) * ext_patches + all_patches + halo_patches
    next_row = jnp.where(
        all_patches >= per_tile - halo_patches,
        (((rel_x + 1) % size_x) * size_y + rel_y) * ext_patches
        + all_patches
        - (per_tile - halo_patches),
        -1,
    )
    prev_row = jnp.where(
        all_patches < halo_patches,
        (((rel_x - 1) % size_x) * size_y + rel_y) * ext_patches
        + all_patches
        + per_tile
        + halo_patches,
        -1,
    )
    row_ids = jnp.arange(tiles * ext_patches, dtype=jnp.int32)[:, None]
    onehot = (
        (own_row[None, :] == row_ids) | (next_row[None, :] == row_ids) | (prev_row[None, :] == row_ids)
    ).astype(jnp.bfloat16)
    table = jnp.einsum("rw,wlpc->rlpc", onehot, rows_in, preferred_element_type=jnp.float32)
    flat = table.reshape(size_x, size_y * ext_patches, levels, patch_rows, patch_cols)

    part = flat[0]
    for step in range(1, size_x):
        part = part + shifted(flat[step], "gx", size_x, step)
    part = part.reshape(size_y, ext_patches, levels, patch_rows, patch_cols)
    left = jnp.roll(part, 1, axis=0)[..., patch_cols - h :]
    right = jnp.roll(part, -1, axis=0)[..., :h]
    strips = jnp.concatenate([left, right], axis=-1)
    packed = jnp.concatenate(
        [part.reshape(size_y, -1), strips.reshape(size_y, -1)], axis=1
    ).reshape(size_y, -1, 128)
    total = packed[0]
    for step in range(1, size_y):
        total = total + shifted(packed[step], "gy", size_y, step)
    other = shifted(total, "group", size_g, 1)
    grad_flat = jnp.where(is_grad, total, other).reshape(-1)
    illum_flat = jnp.where(is_grad, other, total).reshape(-1)

    def unpack(values):
        main_size = ext_patches * levels * patch_rows * patch_cols
        main = values[:main_size].reshape(ext_patches, levels, patch_rows, patch_cols)
        sides = values[main_size:].reshape(ext_patches, levels, patch_rows, 2 * h)
        whole_rows = jnp.concatenate([sides[..., :h], main, sides[..., h:]], axis=-1)
        return whole_rows.transpose(1, 0, 2, 3).reshape(levels, ext_rows, ext_cols)

    grad_ext = unpack(grad_flat)
    illum_ext = unpack(illum_flat)
    pos_x = me_x * tile_rows - h + jnp.arange(ext_rows)
    pos_y = me_y * tile_cols - h + jnp.arange(ext_cols)
    inside = ((pos_x >= 0) & (pos_x < size_x * tile_rows))[:, None] & (
        (pos_y >= 0) & (pos_y < size_y * tile_cols)
    )[None, :]
    field_now = jnp.where(inside, grad_ext / (illum_ext + damping), 0.0)
    for sweep_index in range(SWEEPS):
        padded = jnp.pad(field_now, 1)
        beside = (
            (padded[1:-1, 2:, 1:-1] + padded[1:-1, :-2, 1:-1])
            + (padded[1:-1, 1:-1, 2:] + padded[1:-1, 1:-1, :-2])
            + (padded[2:, 1:-1, 1:-1] + padded[:-2, 1:-1, 1:-1])
        )
        field_now = jnp.where(inside, field_now + smooth_rate * (beside - 6.0 * field_now), 0.0)
    updated_model = velocity - step_length * field_now[:, h : h + tile_rows, h : h + tile_cols]

    tile_table = (
        updated_model.reshape(levels, per_tile, patch_rows, tile_cols)
        .transpose(1, 0, 2, 3)
        .astype(jnp.bfloat16)
    )
    along_y = jnp.stack(
        [tile_table] + [shifted(tile_table, "gy", size_y, step) for step in range(1, size_y)]
    )
    along_x = jnp.stack(
        [along_y] + [shifted(along_y, "gx", size_x, step) for step in range(1, size_x)]
    )
    whole = along_x.reshape(tiles * per_tile, levels, patch_rows, patch_cols)
    owner_x = owners // size_y
    owner_y = owners % size_y
    back_row = (
        ((me_x - owner_x) % size_x) * size_y + (me_y - owner_y) % size_y
    ) * per_tile + patches
    pick = (back_row[:, None] == jnp.arange(tiles * per_tile, dtype=jnp.int32)[None, :]).astype(
        jnp.bfloat16
    )
    returned = jnp.einsum("wr,rlpc->wlpc", pick, whole, preferred_element_type=jnp.float32).astype(
        jnp.bfloat16
    )
    returned_windows = returned.reshape((1, 1, 1, slot_count, levels, patch_rows, patch_cols))
    return (updated_model, returned_windows)


def solution(mesh):
    return jax.shard_map(
        local,
        mesh=mesh,
        in_specs=(
            P("group", "gx", "gy", None, None, None, None),
            P("group", "gx", "gy", None, None, None, None),
            P("group", "gx", "gy", None),
            P("group", "gx", "gy", None),
            P(None, "gx", "gy"),
        ),
        out_specs=(P(None, "gx", "gy"), P("group", "gx", "gy", None, None, None, None)),
        check_vma=False,
    )
```

```python
import jax
import jax.numpy as jnp
from jax import lax
from jax.sharding import PartitionSpec as P

SWEEPS = 4
HALO = SWEEPS


damping = 10.0
smooth_rate = 0.12
step_length = 24.0


def shifted(value, axis, count, step):
    return lax.ppermute(value, axis, [(s, (s + step) % count) for s in range(count)])


def far_first(count):
    steps = list(range(1, count))
    if count % 2 == 0:
        steps.remove(count // 2)
        steps.append(count // 2)
    return steps


def local(gradient_windows, illumination_windows, window_owners, window_patches, velocity):
    size_x = lax.axis_size("gx")
    size_y = lax.axis_size("gy")
    size_g = lax.axis_size("group")
    me_x = lax.axis_index("gx")
    me_y = lax.axis_index("gy")
    slot_grad = gradient_windows[0, 0, 0]
    slot_illum = illumination_windows[0, 0, 0]
    owners = window_owners[0, 0, 0]
    patches = window_patches[0, 0, 0]
    slot_count, levels, patch_rows, patch_cols = slot_grad.shape
    tile_rows, tile_cols = velocity.shape[1], velocity.shape[2]
    per_tile = tile_rows // patch_rows
    tiles = size_x * size_y
    cell_count = levels * patch_rows * patch_cols
    h = HALO
    ext_rows = tile_rows + 2 * h
    ext_cols = tile_cols + 2 * h

    me_g = lax.axis_index("group")
    is_grad = me_g == 0
    kept = jnp.where(is_grad, slot_grad, slot_illum)
    given = jnp.where(is_grad, slot_illum, slot_grad)
    places = jnp.stack([owners, patches])
    taken = shifted(given, "group", size_g, 1)
    taken_places = shifted(places, "group", size_g, 1)
    rows_in = jnp.concatenate([kept, taken], axis=0)
    all_owners = jnp.concatenate([owners, taken_places[0]])
    all_patches = jnp.concatenate([patches, taken_places[1]])

    halo_patches = h // patch_rows
    ext_patches = per_tile + 2 * halo_patches
    rel_x = (all_owners // size_y - me_x) % size_x
    rel_y = (all_owners % size_y - me_y) % size_y
    own_row = (rel_x * size_y + rel_y) * ext_patches + all_patches + halo_patches
    next_row = jnp.where(
        all_patches >= per_tile - halo_patches,
        (((rel_x + 1) % size_x) * size_y + rel_y) * ext_patches
        + all_patches
        - (per_tile - halo_patches),
        -1,
    )
    prev_row = jnp.where(
        all_patches < halo_patches,
        (((rel_x - 1) % size_x) * size_y + rel_y) * ext_patches
        + all_patches
        + per_tile
        + halo_patches,
        -1,
    )
    row_ids = jnp.arange(tiles * ext_patches, dtype=jnp.int32)[:, None]
    onehot = (
        (own_row[None, :] == row_ids) | (next_row[None, :] == row_ids) | (prev_row[None, :] == row_ids)
    ).astype(jnp.bfloat16)
    table = jnp.einsum("rw,wlpc->rlpc", onehot, rows_in, preferred_element_type=jnp.float32)
    flat = table.reshape(size_x, size_y * ext_patches, levels, patch_rows, patch_cols)

    part = flat[0]
    for step in far_first(size_x):
        part = part + shifted(flat[step], "gx", size_x, step)
    part = part.reshape(size_y, ext_patches, levels, patch_rows, patch_cols)
    left = jnp.roll(part, 1, axis=0)[..., patch_cols - h :]
    right = jnp.roll(part, -1, axis=0)[..., :h]
    strips = jnp.concatenate([left, right], axis=-1)
    packed = jnp.concatenate(
        [part.reshape(size_y, -1), strips.reshape(size_y, -1)], axis=1
    ).reshape(size_y, -1, 128)
    total = packed[0]
    for step in range(1, size_y):
        total = total + shifted(packed[step], "gy", size_y, step)
    other = shifted(total, "group", size_g, 1)
    grad_flat = jnp.where(is_grad, total, other).reshape(-1)
    illum_flat = jnp.where(is_grad, other, total).reshape(-1)

    def unpack(values):
        main_size = ext_patches * levels * patch_rows * patch_cols
        main = values[:main_size].reshape(ext_patches, levels, patch_rows, patch_cols)
        sides = values[main_size:].reshape(ext_patches, levels, patch_rows, 2 * h)
        whole_rows = jnp.concatenate([sides[..., :h], main, sides[..., h:]], axis=-1)
        return whole_rows.transpose(1, 0, 2, 3).reshape(levels, ext_rows, ext_cols)

    grad_ext = unpack(grad_flat)
    illum_ext = unpack(illum_flat)
    pos_x = me_x * tile_rows - h + jnp.arange(ext_rows)
    pos_y = me_y * tile_cols - h + jnp.arange(ext_cols)
    inside = ((pos_x >= 0) & (pos_x < size_x * tile_rows))[:, None] & (
        (pos_y >= 0) & (pos_y < size_y * tile_cols)
    )[None, :]
    field_now = jnp.where(inside, grad_ext / (illum_ext + damping), 0.0)
    for sweep_index in range(SWEEPS):
        padded = jnp.pad(field_now, 1)
        beside = (
            (padded[1:-1, 2:, 1:-1] + padded[1:-1, :-2, 1:-1])
            + (padded[1:-1, 1:-1, 2:] + padded[1:-1, 1:-1, :-2])
            + (padded[2:, 1:-1, 1:-1] + padded[:-2, 1:-1, 1:-1])
        )
        field_now = jnp.where(inside, field_now + smooth_rate * (beside - 6.0 * field_now), 0.0)
    updated_model = velocity - step_length * field_now[:, h : h + tile_rows, h : h + tile_cols]

    tile_table = (
        updated_model.reshape(levels, per_tile, patch_rows, tile_cols)
        .transpose(1, 0, 2, 3)
        .astype(jnp.bfloat16)
    )
    along_y = jnp.stack(
        [tile_table] + [shifted(tile_table, "gy", size_y, step) for step in range(1, size_y)]
    )
    arrived_x = {step: shifted(along_y, "gx", size_x, step) for step in far_first(size_x)}
    along_x = jnp.stack([along_y] + [arrived_x[step] for step in range(1, size_x)])
    whole = along_x.reshape(tiles * per_tile, levels, patch_rows, patch_cols)
    owner_x = owners // size_y
    owner_y = owners % size_y
    back_row = (
        ((me_x - owner_x) % size_x) * size_y + (me_y - owner_y) % size_y
    ) * per_tile + patches
    pick = (back_row[:, None] == jnp.arange(tiles * per_tile, dtype=jnp.int32)[None, :]).astype(
        jnp.bfloat16
    )
    returned = jnp.einsum("wr,rlpc->wlpc", pick, whole, preferred_element_type=jnp.float32).astype(
        jnp.bfloat16
    )
    returned_windows = returned.reshape((1, 1, 1, slot_count, levels, patch_rows, patch_cols))
    return (updated_model, returned_windows)


def solution(mesh):
    return jax.shard_map(
        local,
        mesh=mesh,
        in_specs=(
            P("group", "gx", "gy", None, None, None, None),
            P("group", "gx", "gy", None, None, None, None),
            P("group", "gx", "gy", None),
            P("group", "gx", "gy", None),
            P(None, "gx", "gy"),
        ),
        out_specs=(P(None, "gx", "gy"), P("group", "gx", "gy", None, None, None, None)),
        check_vma=False,
    )
```

```python
import jax
import jax.numpy as jnp
from jax import lax
from jax.sharding import PartitionSpec as P

SWEEPS = 4
HALO = SWEEPS


damping = 10.0
smooth_rate = 0.12
step_length = 24.0


def shifted(value, axis, count, step):
    return lax.ppermute(value, axis, [(s, (s + step) % count) for s in range(count)])


def local(gradient_windows, illumination_windows, window_owners, window_patches, velocity):
    size_x = lax.axis_size("gx")
    size_y = lax.axis_size("gy")
    size_g = lax.axis_size("group")
    me_x = lax.axis_index("gx")
    me_y = lax.axis_index("gy")
    slot_grad = gradient_windows[0, 0, 0]
    slot_illum = illumination_windows[0, 0, 0]
    owners = window_owners[0, 0, 0]
    patches = window_patches[0, 0, 0]
    slot_count, levels, patch_rows, patch_cols = slot_grad.shape
    tile_rows, tile_cols = velocity.shape[1], velocity.shape[2]
    per_tile = tile_rows // patch_rows
    tiles = size_x * size_y
    cell_count = levels * patch_rows * patch_cols
    h = HALO
    ext_rows = tile_rows + 2 * h
    ext_cols = tile_cols + 2 * h

    me_g = lax.axis_index("group")
    is_grad = me_g == 0
    kept = jnp.where(is_grad, slot_grad, slot_illum)
    given = jnp.where(is_grad, slot_illum, slot_grad)
    all_owners = owners
    all_patches = patches

    halo_patches = h // patch_rows
    ext_patches = per_tile + 2 * halo_patches
    rel_x = (all_owners // size_y - me_x) % size_x
    rel_y = (all_owners % size_y - me_y) % size_y
    own_row = (rel_x * size_y + rel_y) * ext_patches + all_patches + halo_patches
    next_row = jnp.where(
        all_patches >= per_tile - halo_patches,
        (((rel_x + 1) % size_x) * size_y + rel_y) * ext_patches
        + all_patches
        - (per_tile - halo_patches),
        -1,
    )
    prev_row = jnp.where(
        all_patches < halo_patches,
        (((rel_x - 1) % size_x) * size_y + rel_y) * ext_patches
        + all_patches
        + per_tile
        + halo_patches,
        -1,
    )
    row_ids = jnp.arange(tiles * ext_patches, dtype=jnp.int32)[:, None]
    onehot = (
        (own_row[None, :] == row_ids) | (next_row[None, :] == row_ids) | (prev_row[None, :] == row_ids)
    ).astype(jnp.bfloat16)
    for_partner = jnp.einsum("rw,wlpc->rlpc", onehot, given, preferred_element_type=jnp.float32)
    table = jnp.einsum(
        "rw,wlpc->rlpc", onehot, kept, preferred_element_type=jnp.float32
    ) + shifted(for_partner, "group", size_g, 1)
    flat = table.reshape(size_x, size_y * ext_patches, levels, patch_rows, patch_cols)

    part = flat[0]
    for step in range(1, size_x):
        part = part + shifted(flat[step], "gx", size_x, step)
    part = part.reshape(size_y, ext_patches, levels, patch_rows, patch_cols)
    left = jnp.roll(part, 1, axis=0)[..., patch_cols - h :]
    right = jnp.roll(part, -1, axis=0)[..., :h]
    strips = jnp.concatenate([left, right], axis=-1)
    packed = jnp.concatenate(
        [part.reshape(size_y, -1), strips.reshape(size_y, -1)], axis=1
    ).reshape(size_y, -1, 128)
    total = packed[0]
    for step in range(1, size_y):
        total = total + shifted(packed[step], "gy", size_y, step)
    other = shifted(total, "group", size_g, 1)
    grad_flat = jnp.where(is_grad, total, other).reshape(-1)
    illum_flat = jnp.where(is_grad, other, total).reshape(-1)

    def unpack(values):
        main_size = ext_patches * levels * patch_rows * patch_cols
        main = values[:main_size].reshape(ext_patches, levels, patch_rows, patch_cols)
        sides = values[main_size:].reshape(ext_patches, levels, patch_rows, 2 * h)
        whole_rows = jnp.concatenate([sides[..., :h], main, sides[..., h:]], axis=-1)
        return whole_rows.transpose(1, 0, 2, 3).reshape(levels, ext_rows, ext_cols)

    grad_ext = unpack(grad_flat)
    illum_ext = unpack(illum_flat)
    pos_x = me_x * tile_rows - h + jnp.arange(ext_rows)
    pos_y = me_y * tile_cols - h + jnp.arange(ext_cols)
    inside = ((pos_x >= 0) & (pos_x < size_x * tile_rows))[:, None] & (
        (pos_y >= 0) & (pos_y < size_y * tile_cols)
    )[None, :]
    field_now = jnp.where(inside, grad_ext / (illum_ext + damping), 0.0)
    for sweep_index in range(SWEEPS):
        padded = jnp.pad(field_now, 1)
        beside = (
            (padded[1:-1, 2:, 1:-1] + padded[1:-1, :-2, 1:-1])
            + (padded[1:-1, 1:-1, 2:] + padded[1:-1, 1:-1, :-2])
            + (padded[2:, 1:-1, 1:-1] + padded[:-2, 1:-1, 1:-1])
        )
        field_now = jnp.where(inside, field_now + smooth_rate * (beside - 6.0 * field_now), 0.0)
    updated_model = velocity - step_length * field_now[:, h : h + tile_rows, h : h + tile_cols]

    tile_table = (
        updated_model.reshape(levels, per_tile, patch_rows, tile_cols)
        .transpose(1, 0, 2, 3)
        .astype(jnp.bfloat16)
    )
    along_y = jnp.stack(
        [tile_table] + [shifted(tile_table, "gy", size_y, step) for step in range(1, size_y)]
    )
    along_x = jnp.stack(
        [along_y] + [shifted(along_y, "gx", size_x, step) for step in range(1, size_x)]
    )
    whole = along_x.reshape(tiles * per_tile, levels, patch_rows, patch_cols)
    owner_x = owners // size_y
    owner_y = owners % size_y
    back_row = (
        ((me_x - owner_x) % size_x) * size_y + (me_y - owner_y) % size_y
    ) * per_tile + patches
    pick = (back_row[:, None] == jnp.arange(tiles * per_tile, dtype=jnp.int32)[None, :]).astype(
        jnp.bfloat16
    )
    returned = jnp.einsum("wr,rlpc->wlpc", pick, whole, preferred_element_type=jnp.float32).astype(
        jnp.bfloat16
    )
    returned_windows = returned.reshape((1, 1, 1, slot_count, levels, patch_rows, patch_cols))
    return (updated_model, returned_windows)


def solution(mesh):
    return jax.shard_map(
        local,
        mesh=mesh,
        in_specs=(
            P("group", "gx", "gy", None, None, None, None),
            P("group", "gx", "gy", None, None, None, None),
            P("group", "gx", "gy", None),
            P("group", "gx", "gy", None),
            P(None, "gx", "gy"),
        ),
        out_specs=(P(None, "gx", "gy"), P("group", "gx", "gy", None, None, None, None)),
        check_vma=False,
    )
```

```python
import jax
import jax.numpy as jnp
from jax import lax
from jax.sharding import PartitionSpec as P

SWEEPS = 4
HALO = SWEEPS


damping = 10.0
smooth_rate = 0.12
step_length = 24.0


def shifted(value, axis, count, step):
    return lax.ppermute(value, axis, [(s, (s + step) % count) for s in range(count)])


def local(gradient_windows, illumination_windows, window_owners, window_patches, velocity):
    size_x = lax.axis_size("gx")
    size_y = lax.axis_size("gy")
    size_g = lax.axis_size("group")
    me_x = lax.axis_index("gx")
    me_y = lax.axis_index("gy")
    slot_grad = gradient_windows[0, 0, 0]
    slot_illum = illumination_windows[0, 0, 0]
    owners = window_owners[0, 0, 0]
    patches = window_patches[0, 0, 0]
    slot_count, levels, patch_rows, patch_cols = slot_grad.shape
    tile_rows, tile_cols = velocity.shape[1], velocity.shape[2]
    per_tile = tile_rows // patch_rows
    tiles = size_x * size_y
    cell_count = levels * patch_rows * patch_cols
    h = HALO
    ext_rows = tile_rows + 2 * h
    ext_cols = tile_cols + 2 * h

    me_g = lax.axis_index("group")
    is_grad = me_g == 0
    kept = jnp.where(is_grad, slot_grad, slot_illum)
    given = jnp.where(is_grad, slot_illum, slot_grad)
    places = jnp.stack([owners, patches])
    taken = shifted(given, "group", size_g, 1)
    taken_places = shifted(places, "group", size_g, 1)
    rows_in = jnp.concatenate([kept, taken], axis=0)
    all_owners = jnp.concatenate([owners, taken_places[0]])
    all_patches = jnp.concatenate([patches, taken_places[1]])

    halo_patches = h // patch_rows
    ext_patches = per_tile + 2 * halo_patches
    rel_x = (all_owners // size_y - me_x) % size_x
    rel_y = (all_owners % size_y - me_y) % size_y
    own_row = (rel_x * size_y + rel_y) * ext_patches + all_patches + halo_patches
    next_row = jnp.where(
        all_patches >= per_tile - halo_patches,
        (((rel_x + 1) % size_x) * size_y + rel_y) * ext_patches
        + all_patches
        - (per_tile - halo_patches),
        -1,
    )
    prev_row = jnp.where(
        all_patches < halo_patches,
        (((rel_x - 1) % size_x) * size_y + rel_y) * ext_patches
        + all_patches
        + per_tile
        + halo_patches,
        -1,
    )
    row_ids = jnp.arange(tiles * ext_patches, dtype=jnp.int32)[:, None]
    onehot = (
        (own_row[None, :] == row_ids) | (next_row[None, :] == row_ids) | (prev_row[None, :] == row_ids)
    ).astype(jnp.bfloat16)
    table = jnp.einsum("rw,wlpc->rlpc", onehot, rows_in, preferred_element_type=jnp.float32)
    flat = table.reshape(size_x, size_y * ext_patches, levels, patch_rows, patch_cols)

    part = flat[0]
    for step in range(1, size_x):
        part = part + shifted(flat[step], "gx", size_x, step)
    part = part.reshape(size_y, ext_patches, levels, patch_rows, patch_cols)
    left = jnp.roll(part, 1, axis=0)[..., patch_cols - h :]
    right = jnp.roll(part, -1, axis=0)[..., :h]
    strips = jnp.concatenate([left, right], axis=-1)
    packed = jnp.concatenate(
        [part.reshape(size_y, -1), strips.reshape(size_y, -1)], axis=1
    ).reshape(size_y, -1, 128)
    total = packed[0]
    for step in range(1, size_y):
        total = total + shifted(packed[step], "gy", size_y, step)
    other = shifted(total, "group", size_g, 1)
    grad_flat = jnp.where(is_grad, total, other).reshape(-1)
    illum_flat = jnp.where(is_grad, other, total).reshape(-1)

    def unpack(values):
        main_size = ext_patches * levels * patch_rows * patch_cols
        main = values[:main_size].reshape(ext_patches, levels, patch_rows, patch_cols)
        sides = values[main_size:].reshape(ext_patches, levels, patch_rows, 2 * h)
        whole_rows = jnp.concatenate([sides[..., :h], main, sides[..., h:]], axis=-1)
        return whole_rows.transpose(1, 0, 2, 3).reshape(levels, ext_rows, ext_cols)

    precondition = unpack(grad_flat / (illum_flat + damping))
    pos_x = me_x * tile_rows - h + jnp.arange(ext_rows)
    pos_y = me_y * tile_cols - h + jnp.arange(ext_cols)
    inside = ((pos_x >= 0) & (pos_x < size_x * tile_rows))[:, None] & (
        (pos_y >= 0) & (pos_y < size_y * tile_cols)
    )[None, :]
    field_now = jnp.where(inside, precondition, 0.0)
    for sweep_index in range(SWEEPS):
        padded = jnp.pad(field_now, 1)
        beside = (
            (padded[1:-1, 2:, 1:-1] + padded[1:-1, :-2, 1:-1])
            + (padded[1:-1, 1:-1, 2:] + padded[1:-1, 1:-1, :-2])
            + (padded[2:, 1:-1, 1:-1] + padded[:-2, 1:-1, 1:-1])
        )
        field_now = jnp.where(inside, field_now + smooth_rate * (beside - 6.0 * field_now), 0.0)
    updated_model = velocity - step_length * field_now[:, h : h + tile_rows, h : h + tile_cols]

    tile_table = (
        updated_model.reshape(levels, per_tile, patch_rows, tile_cols)
        .transpose(1, 0, 2, 3)
        .astype(jnp.bfloat16)
    )
    along_y = jnp.stack(
        [tile_table] + [shifted(tile_table, "gy", size_y, step) for step in range(1, size_y)]
    )
    along_x = jnp.stack(
        [along_y] + [shifted(along_y, "gx", size_x, step) for step in range(1, size_x)]
    )
    whole = along_x.reshape(tiles * per_tile, levels, patch_rows, patch_cols)
    owner_x = owners // size_y
    owner_y = owners % size_y
    back_row = (
        ((me_x - owner_x) % size_x) * size_y + (me_y - owner_y) % size_y
    ) * per_tile + patches
    pick = (back_row[:, None] == jnp.arange(tiles * per_tile, dtype=jnp.int32)[None, :]).astype(
        jnp.bfloat16
    )
    returned = jnp.einsum("wr,rlpc->wlpc", pick, whole, preferred_element_type=jnp.float32).astype(
        jnp.bfloat16
    )
    returned_windows = returned.reshape((1, 1, 1, slot_count, levels, patch_rows, patch_cols))
    return (updated_model, returned_windows)


def solution(mesh):
    return jax.shard_map(
        local,
        mesh=mesh,
        in_specs=(
            P("group", "gx", "gy", None, None, None, None),
            P("group", "gx", "gy", None, None, None, None),
            P("group", "gx", "gy", None),
            P("group", "gx", "gy", None),
            P(None, "gx", "gy"),
        ),
        out_specs=(P(None, "gx", "gy"), P("group", "gx", "gy", None, None, None, None)),
        check_vma=False,
    )
```

```python
import jax
import jax.numpy as jnp
from jax import lax
from jax.sharding import PartitionSpec as P
from jax.experimental import pallas as pl
from jax.experimental.pallas import tpu as pltpu

SWEEPS = 4
HALO = SWEEPS


damping = 10.0
smooth_rate = 0.12
step_length = 24.0


def shifted(value, axis, count, step):
    return lax.ppermute(value, axis, [(s, (s + step) % count) for s in range(count)])


def sweeps_kernel(field_ref, inside_ref, out_ref):
    inside = inside_ref[...] > 0.5
    field_now = field_ref[...]
    rows = field_now.shape[1]
    cols = field_now.shape[2]
    no_level = jnp.zeros_like(field_now[:1])
    for sweep_index in range(SWEEPS):
        beside = (
            (pltpu.roll(field_now, rows - 1, 1) + pltpu.roll(field_now, 1, 1))
            + (pltpu.roll(field_now, cols - 1, 2) + pltpu.roll(field_now, 1, 2))
            + (
                jnp.concatenate([field_now[1:], no_level], axis=0)
                + jnp.concatenate([no_level, field_now[:-1]], axis=0)
            )
        )
        field_now = jnp.where(inside, field_now + smooth_rate * (beside - 6.0 * field_now), 0.0)
    out_ref[...] = field_now


def local(gradient_windows, illumination_windows, window_owners, window_patches, velocity):
    size_x = lax.axis_size("gx")
    size_y = lax.axis_size("gy")
    size_g = lax.axis_size("group")
    me_x = lax.axis_index("gx")
    me_y = lax.axis_index("gy")
    slot_grad = gradient_windows[0, 0, 0]
    slot_illum = illumination_windows[0, 0, 0]
    owners = window_owners[0, 0, 0]
    patches = window_patches[0, 0, 0]
    slot_count, levels, patch_rows, patch_cols = slot_grad.shape
    tile_rows, tile_cols = velocity.shape[1], velocity.shape[2]
    per_tile = tile_rows // patch_rows
    tiles = size_x * size_y
    cell_count = levels * patch_rows * patch_cols
    h = HALO
    ext_rows = tile_rows + 2 * h
    ext_cols = tile_cols + 2 * h

    me_g = lax.axis_index("group")
    is_grad = me_g == 0
    kept = jnp.where(is_grad, slot_grad, slot_illum)
    given = jnp.where(is_grad, slot_illum, slot_grad)
    places = jnp.stack([owners, patches])
    taken = shifted(given, "group", size_g, 1)
    taken_places = shifted(places, "group", size_g, 1)
    rows_in = jnp.concatenate([kept, taken], axis=0)
    all_owners = jnp.concatenate([owners, taken_places[0]])
    all_patches = jnp.concatenate([patches, taken_places[1]])

    halo_patches = h // patch_rows
    ext_patches = per_tile + 2 * halo_patches
    rel_x = (all_owners // size_y - me_x) % size_x
    rel_y = (all_owners % size_y - me_y) % size_y
    own_row = (rel_x * size_y + rel_y) * ext_patches + all_patches + halo_patches
    next_row = jnp.where(
        all_patches >= per_tile - halo_patches,
        (((rel_x + 1) % size_x) * size_y + rel_y) * ext_patches
        + all_patches
        - (per_tile - halo_patches),
        -1,
    )
    prev_row = jnp.where(
        all_patches < halo_patches,
        (((rel_x - 1) % size_x) * size_y + rel_y) * ext_patches
        + all_patches
        + per_tile
        + halo_patches,
        -1,
    )
    row_ids = jnp.arange(tiles * ext_patches, dtype=jnp.int32)[:, None]
    onehot = (
        (own_row[None, :] == row_ids) | (next_row[None, :] == row_ids) | (prev_row[None, :] == row_ids)
    ).astype(jnp.bfloat16)
    table = jnp.einsum("rw,wlpc->rlpc", onehot, rows_in, preferred_element_type=jnp.float32)
    flat = table.reshape(size_x, size_y * ext_patches, levels, patch_rows, patch_cols)

    part = flat[0]
    for step in range(1, size_x):
        part = part + shifted(flat[step], "gx", size_x, step)
    part = part.reshape(size_y, ext_patches, levels, patch_rows, patch_cols)
    left = jnp.roll(part, 1, axis=0)[..., patch_cols - h :]
    right = jnp.roll(part, -1, axis=0)[..., :h]
    strips = jnp.concatenate([left, right], axis=-1)
    packed = jnp.concatenate(
        [part.reshape(size_y, -1), strips.reshape(size_y, -1)], axis=1
    ).reshape(size_y, -1, 128)
    total = packed[0]
    for step in range(1, size_y):
        total = total + shifted(packed[step], "gy", size_y, step)
    other = shifted(total, "group", size_g, 1)
    grad_flat = jnp.where(is_grad, total, other).reshape(-1)
    illum_flat = jnp.where(is_grad, other, total).reshape(-1)

    def unpack(values):
        main_size = ext_patches * levels * patch_rows * patch_cols
        main = values[:main_size].reshape(ext_patches, levels, patch_rows, patch_cols)
        sides = values[main_size:].reshape(ext_patches, levels, patch_rows, 2 * h)
        whole_rows = jnp.concatenate([sides[..., :h], main, sides[..., h:]], axis=-1)
        return whole_rows.transpose(1, 0, 2, 3).reshape(levels, ext_rows, ext_cols)

    grad_ext = unpack(grad_flat)
    illum_ext = unpack(illum_flat)
    pos_x = me_x * tile_rows - h + jnp.arange(ext_rows)
    pos_y = me_y * tile_cols - h + jnp.arange(ext_cols)
    inside = ((pos_x >= 0) & (pos_x < size_x * tile_rows))[:, None] & (
        (pos_y >= 0) & (pos_y < size_y * tile_cols)
    )[None, :]
    lanes = -(-ext_cols // 128) * 128
    inside_wide = jnp.pad(inside, ((0, 0), (0, lanes - ext_cols))).astype(jnp.float32)
    start = jnp.pad(
        jnp.where(inside, grad_ext / (illum_ext + damping), 0.0),
        ((0, 0), (0, 0), (0, lanes - ext_cols)),
    )
    field_now = pl.pallas_call(
        sweeps_kernel,
        out_shape=jax.ShapeDtypeStruct(start.shape, jnp.float32),
        in_specs=[pl.BlockSpec(memory_space=pltpu.VMEM)] * 2,
        out_specs=pl.BlockSpec(memory_space=pltpu.VMEM),
    )(start, inside_wide)
    updated_model = velocity - step_length * field_now[:, h : h + tile_rows, h : h + tile_cols]

    tile_table = (
        updated_model.reshape(levels, per_tile, patch_rows, tile_cols)
        .transpose(1, 0, 2, 3)
        .astype(jnp.bfloat16)
    )
    along_y = jnp.stack(
        [tile_table] + [shifted(tile_table, "gy", size_y, step) for step in range(1, size_y)]
    )
    along_x = jnp.stack(
        [along_y] + [shifted(along_y, "gx", size_x, step) for step in range(1, size_x)]
    )
    whole = along_x.reshape(tiles * per_tile, levels, patch_rows, patch_cols)
    owner_x = owners // size_y
    owner_y = owners % size_y
    back_row = (
        ((me_x - owner_x) % size_x) * size_y + (me_y - owner_y) % size_y
    ) * per_tile + patches
    pick = (back_row[:, None] == jnp.arange(tiles * per_tile, dtype=jnp.int32)[None, :]).astype(
        jnp.bfloat16
    )
    returned = jnp.einsum("wr,rlpc->wlpc", pick, whole, preferred_element_type=jnp.float32).astype(
        jnp.bfloat16
    )
    returned_windows = returned.reshape((1, 1, 1, slot_count, levels, patch_rows, patch_cols))
    return (updated_model, returned_windows)


def solution(mesh):
    return jax.shard_map(
        local,
        mesh=mesh,
        in_specs=(
            P("group", "gx", "gy", None, None, None, None),
            P("group", "gx", "gy", None, None, None, None),
            P("group", "gx", "gy", None),
            P("group", "gx", "gy", None),
            P(None, "gx", "gy"),
        ),
        out_specs=(P(None, "gx", "gy"), P("group", "gx", "gy", None, None, None, None)),
        check_vma=False,
    )
```

```python
import jax
import jax.numpy as jnp
from jax import lax
from jax.sharding import PartitionSpec as P

SWEEPS = 4
HALO = SWEEPS


damping = 10.0
smooth_rate = 0.12
step_length = 24.0


def shifted(value, axis, count, step):
    return lax.ppermute(value, axis, [(s, (s + step) % count) for s in range(count)])


def local(gradient_windows, illumination_windows, window_owners, window_patches, velocity):
    size_x = lax.axis_size("gx")
    size_y = lax.axis_size("gy")
    size_g = lax.axis_size("group")
    me_x = lax.axis_index("gx")
    me_y = lax.axis_index("gy")
    slot_grad = gradient_windows[0, 0, 0]
    slot_illum = illumination_windows[0, 0, 0]
    owners = window_owners[0, 0, 0]
    patches = window_patches[0, 0, 0]
    slot_count, levels, patch_rows, patch_cols = slot_grad.shape
    tile_rows, tile_cols = velocity.shape[1], velocity.shape[2]
    per_tile = tile_rows // patch_rows
    tiles = size_x * size_y
    cell_count = levels * patch_rows * patch_cols
    h = HALO
    ext_rows = tile_rows + 2 * h
    ext_cols = tile_cols + 2 * h

    me_g = lax.axis_index("group")
    is_grad = me_g == 0
    given = jnp.where(is_grad, slot_illum, slot_grad)
    places = jnp.stack([owners, patches])
    taken = shifted(given, "group", size_g, 1)
    taken_places = shifted(places, "group", size_g, 1)
    all_owners = jnp.concatenate([owners, taken_places[0]])
    all_patches = jnp.concatenate([patches, taken_places[1]])

    halo_patches = h // patch_rows
    ext_patches = per_tile + 2 * halo_patches
    rel_x = (all_owners // size_y - me_x) % size_x
    rel_y = (all_owners % size_y - me_y) % size_y
    own_row = (rel_x * size_y + rel_y) * ext_patches + all_patches + halo_patches
    next_row = jnp.where(
        all_patches >= per_tile - halo_patches,
        (((rel_x + 1) % size_x) * size_y + rel_y) * ext_patches
        + all_patches
        - (per_tile - halo_patches),
        -1,
    )
    prev_row = jnp.where(
        all_patches < halo_patches,
        (((rel_x - 1) % size_x) * size_y + rel_y) * ext_patches
        + all_patches
        + per_tile
        + halo_patches,
        -1,
    )
    row_ids = jnp.arange(tiles * ext_patches, dtype=jnp.int32)[:, None]
    onehot = (
        (own_row[None, :] == row_ids) | (next_row[None, :] == row_ids) | (prev_row[None, :] == row_ids)
    ).astype(jnp.bfloat16)
    own, theirs = onehot[:, :slot_count], onehot[:, slot_count:]
    zero = jnp.zeros_like(own)
    table = (
        jnp.einsum(
            "rw,wlpc->rlpc", jnp.where(is_grad, own, zero), slot_grad, preferred_element_type=jnp.float32
        )
        + jnp.einsum(
            "rw,wlpc->rlpc", jnp.where(is_grad, zero, own), slot_illum, preferred_element_type=jnp.float32
        )
    ) + jnp.einsum("rw,wlpc->rlpc", theirs, taken, preferred_element_type=jnp.float32)
    flat = table.reshape(size_x, size_y * ext_patches, levels, patch_rows, patch_cols)

    part = flat[0]
    for step in range(1, size_x):
        part = part + shifted(flat[step], "gx", size_x, step)
    part = part.reshape(size_y, ext_patches, levels, patch_rows, patch_cols)
    left = jnp.roll(part, 1, axis=0)[..., patch_cols - h :]
    right = jnp.roll(part, -1, axis=0)[..., :h]
    strips = jnp.concatenate([left, right], axis=-1)
    packed = jnp.concatenate(
        [part.reshape(size_y, -1), strips.reshape(size_y, -1)], axis=1
    ).reshape(size_y, -1, 128)
    total = packed[0]
    for step in range(1, size_y):
        total = total + shifted(packed[step], "gy", size_y, step)
    other = shifted(total, "group", size_g, 1)
    grad_flat = jnp.where(is_grad, total, other).reshape(-1)
    illum_flat = jnp.where(is_grad, other, total).reshape(-1)

    def unpack(values):
        main_size = ext_patches * levels * patch_rows * patch_cols
        main = values[:main_size].reshape(ext_patches, levels, patch_rows, patch_cols)
        sides = values[main_size:].reshape(ext_patches, levels, patch_rows, 2 * h)
        whole_rows = jnp.concatenate([sides[..., :h], main, sides[..., h:]], axis=-1)
        return whole_rows.transpose(1, 0, 2, 3).reshape(levels, ext_rows, ext_cols)

    grad_ext = unpack(grad_flat)
    illum_ext = unpack(illum_flat)
    pos_x = me_x * tile_rows - h + jnp.arange(ext_rows)
    pos_y = me_y * tile_cols - h + jnp.arange(ext_cols)
    inside = ((pos_x >= 0) & (pos_x < size_x * tile_rows))[:, None] & (
        (pos_y >= 0) & (pos_y < size_y * tile_cols)
    )[None, :]
    field_now = jnp.where(inside, grad_ext / (illum_ext + damping), 0.0)
    for sweep_index in range(SWEEPS):
        padded = jnp.pad(field_now, 1)
        beside = (
            (padded[1:-1, 2:, 1:-1] + padded[1:-1, :-2, 1:-1])
            + (padded[1:-1, 1:-1, 2:] + padded[1:-1, 1:-1, :-2])
            + (padded[2:, 1:-1, 1:-1] + padded[:-2, 1:-1, 1:-1])
        )
        field_now = jnp.where(inside, field_now + smooth_rate * (beside - 6.0 * field_now), 0.0)
    updated_model = velocity - step_length * field_now[:, h : h + tile_rows, h : h + tile_cols]

    tile_table = (
        updated_model.reshape(levels, per_tile, patch_rows, tile_cols)
        .transpose(1, 0, 2, 3)
        .astype(jnp.bfloat16)
    )
    along_y = jnp.stack(
        [tile_table] + [shifted(tile_table, "gy", size_y, step) for step in range(1, size_y)]
    )
    along_x = jnp.stack(
        [along_y] + [shifted(along_y, "gx", size_x, step) for step in range(1, size_x)]
    )
    whole = along_x.reshape(tiles * per_tile, levels, patch_rows, patch_cols)
    owner_x = owners // size_y
    owner_y = owners % size_y
    back_row = (
        ((me_x - owner_x) % size_x) * size_y + (me_y - owner_y) % size_y
    ) * per_tile + patches
    pick = (back_row[:, None] == jnp.arange(tiles * per_tile, dtype=jnp.int32)[None, :]).astype(
        jnp.bfloat16
    )
    returned = jnp.einsum("wr,rlpc->wlpc", pick, whole, preferred_element_type=jnp.float32).astype(
        jnp.bfloat16
    )
    returned_windows = returned.reshape((1, 1, 1, slot_count, levels, patch_rows, patch_cols))
    return (updated_model, returned_windows)


def solution(mesh):
    return jax.shard_map(
        local,
        mesh=mesh,
        in_specs=(
            P("group", "gx", "gy", None, None, None, None),
            P("group", "gx", "gy", None, None, None, None),
            P("group", "gx", "gy", None),
            P("group", "gx", "gy", None),
            P(None, "gx", "gy"),
        ),
        out_specs=(P(None, "gx", "gy"), P("group", "gx", "gy", None, None, None, None)),
        check_vma=False,
    )
```

```python
import jax
import jax.numpy as jnp
from jax import lax
from jax.sharding import PartitionSpec as P

SWEEPS = 4
HALO = SWEEPS


damping = 10.0
smooth_rate = 0.12
step_length = 24.0


def shifted(value, axis, count, step):
    return lax.ppermute(value, axis, [(s, (s + step) % count) for s in range(count)])


def swapped(value, axis, count, mask):
    return lax.ppermute(value, axis, [(s, s ^ mask) for s in range(count)])


def local(gradient_windows, illumination_windows, window_owners, window_patches, velocity):
    size_x = lax.axis_size("gx")
    size_y = lax.axis_size("gy")
    size_g = lax.axis_size("group")
    me_x = lax.axis_index("gx")
    me_y = lax.axis_index("gy")
    slot_grad = gradient_windows[0, 0, 0]
    slot_illum = illumination_windows[0, 0, 0]
    owners = window_owners[0, 0, 0]
    patches = window_patches[0, 0, 0]
    slot_count, levels, patch_rows, patch_cols = slot_grad.shape
    tile_rows, tile_cols = velocity.shape[1], velocity.shape[2]
    per_tile = tile_rows // patch_rows
    tiles = size_x * size_y
    cell_count = levels * patch_rows * patch_cols
    h = HALO
    ext_rows = tile_rows + 2 * h
    ext_cols = tile_cols + 2 * h

    me_g = lax.axis_index("group")
    is_grad = me_g == 0
    kept = jnp.where(is_grad, slot_grad, slot_illum)
    given = jnp.where(is_grad, slot_illum, slot_grad)
    places = jnp.stack([owners, patches])
    taken = shifted(given, "group", size_g, 1)
    taken_places = shifted(places, "group", size_g, 1)
    rows_in = jnp.concatenate([kept, taken], axis=0)
    all_owners = jnp.concatenate([owners, taken_places[0]])
    all_patches = jnp.concatenate([patches, taken_places[1]])

    halo_patches = h // patch_rows
    ext_patches = per_tile + 2 * halo_patches
    all_x = all_owners // size_y
    rel_x = all_x ^ me_x
    rel_y = (all_owners % size_y) ^ me_y
    own_row = (rel_x * size_y + rel_y) * ext_patches + all_patches + halo_patches
    next_row = jnp.where(
        all_patches >= per_tile - halo_patches,
        ((((all_x + 1) % size_x) ^ me_x) * size_y + rel_y) * ext_patches
        + all_patches
        - (per_tile - halo_patches),
        -1,
    )
    prev_row = jnp.where(
        all_patches < halo_patches,
        ((((all_x - 1) % size_x) ^ me_x) * size_y + rel_y) * ext_patches
        + all_patches
        + per_tile
        + halo_patches,
        -1,
    )
    row_ids = jnp.arange(tiles * ext_patches, dtype=jnp.int32)[:, None]
    onehot = (
        (own_row[None, :] == row_ids) | (next_row[None, :] == row_ids) | (prev_row[None, :] == row_ids)
    ).astype(jnp.bfloat16)
    table = jnp.einsum("rw,wlpc->rlpc", onehot, rows_in, preferred_element_type=jnp.float32)
    flat = table.reshape(size_x, size_y * ext_patches, levels, patch_rows, patch_cols)

    part = flat[0]
    for step in range(1, size_x):
        part = part + swapped(flat[step], "gx", size_x, step)
    part = part.reshape(size_y, ext_patches, levels, patch_rows, patch_cols)
    slot_y = jnp.arange(size_y, dtype=jnp.int32) ^ me_y
    left = jnp.take(part, ((slot_y - 1) % size_y) ^ me_y, axis=0)[..., patch_cols - h :]
    right = jnp.take(part, ((slot_y + 1) % size_y) ^ me_y, axis=0)[..., :h]
    strips = jnp.concatenate([left, right], axis=-1)
    packed = jnp.concatenate(
        [part.reshape(size_y, -1), strips.reshape(size_y, -1)], axis=1
    ).reshape(size_y, -1, 128)
    total = packed[0]
    for step in range(1, size_y):
        total = total + swapped(packed[step], "gy", size_y, step)
    other = shifted(total, "group", size_g, 1)
    grad_flat = jnp.where(is_grad, total, other).reshape(-1)
    illum_flat = jnp.where(is_grad, other, total).reshape(-1)

    def unpack(values):
        main_size = ext_patches * levels * patch_rows * patch_cols
        main = values[:main_size].reshape(ext_patches, levels, patch_rows, patch_cols)
        sides = values[main_size:].reshape(ext_patches, levels, patch_rows, 2 * h)
        whole_rows = jnp.concatenate([sides[..., :h], main, sides[..., h:]], axis=-1)
        return whole_rows.transpose(1, 0, 2, 3).reshape(levels, ext_rows, ext_cols)

    grad_ext = unpack(grad_flat)
    illum_ext = unpack(illum_flat)
    pos_x = me_x * tile_rows - h + jnp.arange(ext_rows)
    pos_y = me_y * tile_cols - h + jnp.arange(ext_cols)
    inside = ((pos_x >= 0) & (pos_x < size_x * tile_rows))[:, None] & (
        (pos_y >= 0) & (pos_y < size_y * tile_cols)
    )[None, :]
    field_now = jnp.where(inside, grad_ext / (illum_ext + damping), 0.0)
    for sweep_index in range(SWEEPS):
        padded = jnp.pad(field_now, 1)
        beside = (
            (padded[1:-1, 2:, 1:-1] + padded[1:-1, :-2, 1:-1])
            + (padded[1:-1, 1:-1, 2:] + padded[1:-1, 1:-1, :-2])
            + (padded[2:, 1:-1, 1:-1] + padded[:-2, 1:-1, 1:-1])
        )
        field_now = jnp.where(inside, field_now + smooth_rate * (beside - 6.0 * field_now), 0.0)
    updated_model = velocity - step_length * field_now[:, h : h + tile_rows, h : h + tile_cols]

    tile_table = (
        updated_model.reshape(levels, per_tile, patch_rows, tile_cols)
        .transpose(1, 0, 2, 3)
        .astype(jnp.bfloat16)
    )
    along_y = jnp.stack(
        [tile_table] + [swapped(tile_table, "gy", size_y, step) for step in range(1, size_y)]
    )
    along_x = jnp.stack(
        [along_y] + [swapped(along_y, "gx", size_x, step) for step in range(1, size_x)]
    )
    whole = along_x.reshape(tiles * per_tile, levels, patch_rows, patch_cols)
    owner_x = owners // size_y
    owner_y = owners % size_y
    back_row = (
        (owner_x ^ me_x) * size_y + (owner_y ^ me_y)
    ) * per_tile + patches
    pick = (back_row[:, None] == jnp.arange(tiles * per_tile, dtype=jnp.int32)[None, :]).astype(
        jnp.bfloat16
    )
    returned = jnp.einsum("wr,rlpc->wlpc", pick, whole, preferred_element_type=jnp.float32).astype(
        jnp.bfloat16
    )
    returned_windows = returned.reshape((1, 1, 1, slot_count, levels, patch_rows, patch_cols))
    return (updated_model, returned_windows)


def solution(mesh):
    return jax.shard_map(
        local,
        mesh=mesh,
        in_specs=(
            P("group", "gx", "gy", None, None, None, None),
            P("group", "gx", "gy", None, None, None, None),
            P("group", "gx", "gy", None),
            P("group", "gx", "gy", None),
            P(None, "gx", "gy"),
        ),
        out_specs=(P(None, "gx", "gy"), P("group", "gx", "gy", None, None, None, None)),
        check_vma=False,
    )
```

```python
import jax
import jax.numpy as jnp
from jax import lax
from jax.sharding import PartitionSpec as P

SWEEPS = 4
HALO = SWEEPS


damping = 10.0
smooth_rate = 0.12
step_length = 24.0


def shifted(value, axis, count, step):
    return lax.ppermute(value, axis, [(s, (s + step) % count) for s in range(count)])


def local(gradient_windows, illumination_windows, window_owners, window_patches, velocity):
    size_x = lax.axis_size("gx")
    size_y = lax.axis_size("gy")
    size_g = lax.axis_size("group")
    me_x = lax.axis_index("gx")
    me_y = lax.axis_index("gy")
    slot_grad = gradient_windows[0, 0, 0]
    slot_illum = illumination_windows[0, 0, 0]
    owners = window_owners[0, 0, 0]
    patches = window_patches[0, 0, 0]
    slot_count, levels, patch_rows, patch_cols = slot_grad.shape
    tile_rows, tile_cols = velocity.shape[1], velocity.shape[2]
    per_tile = tile_rows // patch_rows
    tiles = size_x * size_y
    cell_count = levels * patch_rows * patch_cols
    h = HALO
    ext_rows = tile_rows + 2 * h
    ext_cols = tile_cols + 2 * h

    me_g = lax.axis_index("group")
    is_grad = me_g == 0
    kept = jnp.where(is_grad, slot_grad, slot_illum)
    given = jnp.where(is_grad, slot_illum, slot_grad)
    places = jnp.stack([owners, patches])
    taken = shifted(given, "group", size_g, 1)
    taken_places = shifted(places, "group", size_g, 1)
    rows_in = jnp.concatenate([kept, taken], axis=0)
    all_owners = jnp.concatenate([owners, taken_places[0]])
    all_patches = jnp.concatenate([patches, taken_places[1]])

    halo_patches = h // patch_rows
    ext_patches = per_tile + 2 * halo_patches
    rel_x = (all_owners // size_y - me_x) % size_x
    rel_y = (all_owners % size_y - me_y) % size_y
    own_row = (rel_x * size_y + rel_y) * ext_patches + all_patches + halo_patches
    next_row = jnp.where(
        all_patches >= per_tile - halo_patches,
        (((rel_x + 1) % size_x) * size_y + rel_y) * ext_patches
        + all_patches
        - (per_tile - halo_patches),
        -1,
    )
    prev_row = jnp.where(
        all_patches < halo_patches,
        (((rel_x - 1) % size_x) * size_y + rel_y) * ext_patches
        + all_patches
        + per_tile
        + halo_patches,
        -1,
    )
    row_ids = jnp.arange(tiles * ext_patches, dtype=jnp.int32)[:, None]
    onehot = (
        (own_row[None, :] == row_ids) | (next_row[None, :] == row_ids) | (prev_row[None, :] == row_ids)
    ).astype(jnp.bfloat16)
    table = jnp.einsum("rw,wlpc->rlpc", onehot, rows_in, preferred_element_type=jnp.float32)
    flat = table.reshape(size_x, size_y * ext_patches, levels, patch_rows, patch_cols)

    part = flat[0]
    for step in range(1, size_x):
        part = part + shifted(flat[step], "gx", size_x, step)
    part = part.reshape(size_y, ext_patches, levels, patch_rows, patch_cols)
    left = jnp.roll(part, 1, axis=0)[..., patch_cols - h :]
    right = jnp.roll(part, -1, axis=0)[..., :h]
    strips = jnp.concatenate([left, right], axis=-1)
    packed = jnp.concatenate(
        [part.reshape(size_y, -1), strips.reshape(size_y, -1)], axis=1
    ).reshape(size_y, -1, 128)
    total = packed[0]
    for step in range(1, size_y):
        total = total + shifted(packed[step], "gy", size_y, step)
    other = shifted(total, "group", size_g, 1)
    grad_flat = jnp.where(is_grad, total, other).reshape(-1)
    illum_flat = jnp.where(is_grad, other, total).reshape(-1)

    def unpack(values):
        main_size = ext_patches * levels * patch_rows * patch_cols
        main = values[:main_size].reshape(ext_patches, levels, patch_rows, patch_cols)
        sides = values[main_size:].reshape(ext_patches, levels, patch_rows, 2 * h)
        whole_rows = jnp.concatenate([sides[..., :h], main, sides[..., h:]], axis=-1)
        return whole_rows.transpose(1, 0, 2, 3).reshape(levels, ext_rows, ext_cols)

    grad_ext = unpack(grad_flat)
    illum_ext = unpack(illum_flat)
    pos_x = me_x * tile_rows - h + jnp.arange(ext_rows)
    pos_y = me_y * tile_cols - h + jnp.arange(ext_cols)
    inside = ((pos_x >= 0) & (pos_x < size_x * tile_rows))[:, None] & (
        (pos_y >= 0) & (pos_y < size_y * tile_cols)
    )[None, :]
    field_now = jnp.where(inside, grad_ext / (illum_ext + damping), 0.0)
    for sweep_index in range(SWEEPS):
        padded = jnp.pad(field_now, 1)
        beside = (
            (padded[1:-1, 2:, 1:-1] + padded[1:-1, :-2, 1:-1])
            + (padded[1:-1, 1:-1, 2:] + padded[1:-1, 1:-1, :-2])
            + (padded[2:, 1:-1, 1:-1] + padded[:-2, 1:-1, 1:-1])
        )
        field_now = jnp.where(inside, field_now + smooth_rate * (beside - 6.0 * field_now), 0.0)
    updated_model = velocity - step_length * field_now[:, h : h + tile_rows, h : h + tile_cols]

    tile_table = (
        updated_model.reshape(levels, per_tile, patch_rows, tile_cols)
        .transpose(1, 0, 2, 3)
        .astype(jnp.bfloat16)
    )
    along_x = jnp.stack(
        [tile_table] + [shifted(tile_table, "gx", size_x, step) for step in range(1, size_x)]
    )
    along_y = jnp.stack(
        [along_x] + [shifted(along_x, "gy", size_y, step) for step in range(1, size_y)]
    )
    whole = along_y.reshape(tiles * per_tile, levels, patch_rows, patch_cols)
    owner_x = owners // size_y
    owner_y = owners % size_y
    back_row = (
        ((me_y - owner_y) % size_y) * size_x + (me_x - owner_x) % size_x
    ) * per_tile + patches
    pick = (back_row[:, None] == jnp.arange(tiles * per_tile, dtype=jnp.int32)[None, :]).astype(
        jnp.bfloat16
    )
    returned = jnp.einsum("wr,rlpc->wlpc", pick, whole, preferred_element_type=jnp.float32).astype(
        jnp.bfloat16
    )
    returned_windows = returned.reshape((1, 1, 1, slot_count, levels, patch_rows, patch_cols))
    return (updated_model, returned_windows)


def solution(mesh):
    return jax.shard_map(
        local,
        mesh=mesh,
        in_specs=(
            P("group", "gx", "gy", None, None, None, None),
            P("group", "gx", "gy", None, None, None, None),
            P("group", "gx", "gy", None),
            P("group", "gx", "gy", None),
            P(None, "gx", "gy"),
        ),
        out_specs=(P(None, "gx", "gy"), P("group", "gx", "gy", None, None, None, None)),
        check_vma=False,
    )
```
